32 devices in a mesh: seq: 16 (over z, y, x), grp: 2 (over core).
Axes of the slice: x: 2, y: 2, z: 4, core: 2. Of those that a mesh axis runs over, the one named last changes fastest.
Arguments:
- queries: bfloat16 [4096, 2048], P('seq', 'grp'), parts along dimension 1, may hold values from -80 to 80
- shared_keys: bfloat16 [4096, 256], P('seq', 'grp'), parts along dimension 1, may hold values from -4 to 4
- shared_values: bfloat16 [4096, 256], P('seq', 'grp'), parts along dimension 1, may hold values from -6 to 6
- outputs: bfloat16 [4096, 2048], P('seq', 'grp'), parts along dimension 1, may hold values from -6 to 6
- out_grad: bfloat16 [4096, 2048], P('seq', 'grp'), parts along dimension 1, may hold values from -6 to 6
- doc_lengths: int32 [64], replicated, may hold values from 1 to 2048, 4096 in all
Outputs:
- grad_queries: bfloat16 [4096, 2048], P('seq', 'grp'), parts along dimension 1
- grad_keys: bfloat16 [4096, 256], P('seq', 'grp'), parts along dimension 1
- grad_values: bfloat16 [4096, 256], P('seq', 'grp'), parts along dimension 1
The draws below stay inside these ranges and needn't reach their ends.
There are 2 independent parts, one for each index of `grp`. The reference program is written for one: setup_inputs(seed, part) draws one part's arguments, and reference() takes and returns one part's arrays. A program takes and returns all parts, laid end to end along the dimension named above; an argument that names none is the same for every part. Nothing has to cross between parts.
Inputs may be any that keep to these rules, and one draw needn't show every extreme that they name: `doc_lengths`: lengths of the 64 documents in packing order; they sum to 4096 and the longest is exactly 2048.
All inputs are finite; a program needn't handle non-finite values.
Results may differ from the reference program's by a relative error of at most 0.0051.
Values may be sent and summed in bfloat16 or wider, within the bound.
No kernel may reach another device: no remote copies, remote signals or barrier semaphores. Data moves between devices by JAX's collectives and lax.ppermute only.
A program may use at most 64 MiB of HBM per device.

```python
import math
import jax
import jax.numpy as jnp
import numpy as np
from jax import lax

HEAD = 128
QHEADS = 8
BLOCK = 128
REACH = 16
DOCS = 64
TOKENS = 4096
LONGEST = 2048
N_SEQ = 16


def base_keys(key):
    return jnp.clip(jax.random.normal(jax.random.fold_in(key, 11), (TOKENS, HEAD), jnp.float32), -4.0, 4.0)


def draw_shared_keys(key, part):
    raw_keys = base_keys(key)
    return raw_keys.astype(jnp.bfloat16)


def draw_queries(key, part):
    query_draw = jnp.clip(jax.random.normal(jax.random.fold_in(key, 23), (TOKENS, QHEADS * HEAD), jnp.float32), -5.0, 5.0)
    return query_draw.astype(jnp.bfloat16)


def shard_levels(key, dims, pieces, low, largest):
    loudness, own = 1.0, jax.random.fold_in(key, 6)
    for dim, parts in pieces:
        heights = jnp.exp(jax.random.uniform(jax.random.fold_in(own, dim), (parts,), jnp.float32, low / len(pieces), largest / len(pieces)))
        loudness = loudness * jnp.repeat(heights, dims[dim] // parts).reshape([-1 if axis == dim else 1 for axis in range(len(dims))])
    return loudness


def length_profile(count, total, bound, lean):
    portions = [(1 << 20) // math.isqrt(rank ** lean) + 1 for rank in range(2, count + 1)]
    rest, holding = total - bound - (count - 1), [1] * (count - 1)
    while rest > 0:
        candidates = [i for i in range(count - 1) if holding[i] < bound]
        pool, left = sum([portions[i] for i in candidates]), rest
        for i in candidates:
            more = min(bound - holding[i], max(1, left * portions[i] // pool), rest)
            holding[i] = holding[i] + more
            rest = rest - more
    return np.array([bound] + holding)


def uneven_parts(rng, amount, total, limit, slope):
    if amount == 2:
        one = jax.random.randint(rng, (), max(1, total - limit), min(limit, total - 1) + 1)
        return jnp.stack([one, total - one])
    lengths = jnp.asarray(length_profile(amount, total, limit, slope), jnp.int32)
    twos = (amount - 1) // 2
    source_of, receiver = lengths[1:1 + 2 * twos:2], lengths[2:2 + 2 * twos:2]
    slack = jnp.minimum(source_of - 1, limit - receiver)
    moved = jax.random.randint(jax.random.fold_in(rng, 1), (twos,), 0, 1 << 20) % (slack + 1)
    lengths = lengths.at[1:1 + 2 * twos:2].set(source_of - moved).at[2:2 + 2 * twos:2].set(receiver + moved)
    return lengths[jax.random.permutation(jax.random.fold_in(rng, 2), amount)]


def bell_draw(stream_key, extent, spread, reach, cuts=(), held_as=jnp.bfloat16):
    values = jax.random.normal(stream_key, extent, jnp.float32) * spread
    if len(cuts) > 0:
        values = shard_levels(stream_key, extent, cuts, -0.22, 0.18) * values
    return jnp.clip(values, min=-reach, max=reach).astype(held_as)


def setup_inputs(seed: int = 0, part: int = 0) -> dict:
    arg_keys = jax.random.split(jax.random.key(seed), 7)
    own_keys = jax.random.split(jax.random.fold_in(arg_keys[6], part), 7)
    return {
        "queries": draw_queries(jax.random.fold_in(jax.random.fold_in(arg_keys[6], part), 71), part),
        "shared_keys": draw_shared_keys(jax.random.fold_in(jax.random.fold_in(arg_keys[6], part), 71), part),
        "shared_values": bell_draw(own_keys[2], (TOKENS, HEAD), 1.0, 6.0, ((0, 16),)),
        "outputs": bell_draw(own_keys[3], (TOKENS, QHEADS * HEAD), 1.0, 6.0, ((0, 16),)),
        "out_grad": bell_draw(own_keys[4], (TOKENS, QHEADS * HEAD), 1.0, 6.0, ((0, 16),)),
        "doc_lengths": uneven_parts(arg_keys[5], DOCS, TOKENS, LONGEST, 2).astype(jnp.int32),
    }


def to_sequence(array):
    width_all = array.shape[-1]
    halves = array.reshape(N_SEQ, 2, BLOCK, width_all)
    return jnp.concatenate([halves[:, 0].reshape(-1, width_all), halves[::-1, 1].reshape(-1, width_all)], axis=0)


def to_storage(array):
    width_all = array.shape[-1]
    lower_part = array[: N_SEQ * BLOCK].reshape(N_SEQ, BLOCK, width_all)
    upper_part = array[N_SEQ * BLOCK:].reshape(N_SEQ, BLOCK, width_all)[::-1]
    return jnp.stack([lower_part, upper_part], axis=1).reshape(-1, width_all)


def reference(queries, shared_keys, shared_values, outputs, out_grad, doc_lengths):
    query_seq = to_sequence(queries)
    grad_seq = to_sequence(out_grad)
    out_seq = to_sequence(outputs)
    pair_seq = jnp.concatenate([to_sequence(shared_keys), to_sequence(shared_values)], axis=1)
    doc_ends = jnp.cumsum(doc_lengths).astype(jnp.int32)
    doc_starts = (doc_ends - doc_lengths).astype(jnp.int32)
    positions = jnp.arange(TOKENS, dtype=jnp.int32)
    begins = jnp.max(jnp.where(doc_starts[None, :] <= positions[:, None], doc_starts[None, :], 0), axis=1).astype(jnp.int32)
    pad_rows = REACH * BLOCK
    pair_padded = jnp.concatenate([jnp.zeros((pad_rows, 2 * HEAD), jnp.bfloat16), pair_seq], axis=0)
    window_rows = (REACH + 1) * BLOCK
    scaling = HEAD ** -0.5

    def one_block(key_accum, block_id):
        first_row = (block_id * BLOCK).astype(jnp.int32)
        query_block = lax.dynamic_slice_in_dim(query_seq, first_row, BLOCK, 0).reshape(BLOCK * QHEADS, HEAD)
        grad_block = lax.dynamic_slice_in_dim(grad_seq, first_row, BLOCK, 0).reshape(BLOCK * QHEADS, HEAD)
        out_block = lax.dynamic_slice_in_dim(out_seq, first_row, BLOCK, 0).reshape(BLOCK * QHEADS, HEAD)
        pos_block = jnp.repeat(lax.dynamic_slice_in_dim(positions, first_row, BLOCK, 0), QHEADS)
        begin_block = jnp.repeat(lax.dynamic_slice_in_dim(begins, first_row, BLOCK, 0), QHEADS)
        window = lax.dynamic_slice_in_dim(pair_padded, first_row, window_rows, 0)
        key_pos = first_row - pad_rows + jnp.arange(window_rows, dtype=jnp.int32)
        allowed = (key_pos[None, :] >= begin_block[:, None]) & (key_pos[None, :] <= pos_block[:, None])
        keys_win = window[:, :HEAD]
        values_win = window[:, HEAD:]
        scores = jnp.dot(query_block, keys_win.T, preferred_element_type=jnp.float32) * scaling
        log_total = jax.nn.logsumexp(jnp.where(allowed, scores, -jnp.inf), axis=1)
        attn_probs = jnp.where(allowed, jnp.exp(scores - log_total[:, None]), 0.0)
        probs_low = attn_probs.astype(jnp.bfloat16)
        deltas = jnp.sum(grad_block.astype(jnp.float32) * out_block.astype(jnp.float32), axis=1)
        value_grad = jnp.dot(probs_low.T, grad_block, preferred_element_type=jnp.float32)
        dprobs = jnp.dot(grad_block, values_win.T, preferred_element_type=jnp.float32)
        dscores = (attn_probs * (dprobs - deltas[:, None])).astype(jnp.bfloat16)
        grad_query = (jnp.dot(dscores, keys_win, preferred_element_type=jnp.float32) * scaling).astype(jnp.bfloat16)
        key_grad = jnp.dot(dscores.T, query_block, preferred_element_type=jnp.float32) * scaling
        update = jnp.concatenate([key_grad, value_grad], axis=1)
        current = lax.dynamic_slice_in_dim(key_accum, first_row, window_rows, 0)
        key_accum = lax.dynamic_update_slice_in_dim(key_accum, current + update, first_row, 0)
        return key_accum, grad_query.reshape(BLOCK, QHEADS * HEAD)

    key_accum = jnp.zeros((TOKENS + pad_rows, 2 * HEAD), jnp.float32)
    key_accum, grad_blocks = lax.scan(one_block, key_accum, jnp.arange(2 * N_SEQ, dtype=jnp.int32))
    grad_queries = to_storage(grad_blocks.reshape(TOKENS, QHEADS * HEAD))
    key_sum = key_accum[pad_rows:]
    grad_keys = to_storage(key_sum[:, :HEAD].astype(jnp.bfloat16))
    grad_values = to_storage(key_sum[:, HEAD:].astype(jnp.bfloat16))
    return (grad_queries, grad_keys, grad_values)
```

```python
import functools

import jax
import jax.numpy as jnp
from jax import lax
from jax.experimental import pallas as pl
from jax.experimental.pallas import tpu as pltpu
from jax.sharding import PartitionSpec as P

REACH = 16


def _bwd_kernel(blk_ref, kb0_ref, q_ref, do_ref, kv_ref, kt_ref, begin_ref, qpos_ref,
                delta_ref, dq_ref, dkv_ref, qall, doall, dqt,
                *, rows, heads, width, reach, scaling):
    s = pl.program_id(0)
    b = blk_ref[s]
    kb0 = kb0_ref[s]
    for h in range(heads):
        qall[h * rows:(h + 1) * rows, :] = q_ref[:, h * width:(h + 1) * width]
        doall[h * rows:(h + 1) * rows, :] = do_ref[:, h * width:(h + 1) * width]
    begin = begin_ref[...]
    qpos = qpos_ref[...]
    delta = delta_ref[...]
    dqt[...] = jnp.zeros(dqt.shape, jnp.float32)
    dkv_ref[...] = jnp.zeros(dkv_ref.shape, jnp.float32)
    k_iota = lax.broadcasted_iota(jnp.int32, (rows, 1), 0)
    base = (b - reach) * rows
    nt = (((1,), (1,)), ((), ()))

    def scores(c):
        kc = kv_ref[c, :, :width]
        st = lax.dot_general(kc, qall[...], nt, preferred_element_type=jnp.float32) * scaling
        kpos = base + c * rows + k_iota
        allowed = (kpos >= begin) & (kpos <= qpos)
        return st, allowed

    def stat_step(c, carry):
        m, l = carry
        st, allowed = scores(c)
        masked = jnp.where(allowed, st, -1e30)
        m_new = jnp.maximum(m, jnp.max(masked, axis=0, keepdims=True))
        e = jnp.where(allowed, jnp.exp(st - m_new), 0.0)
        l = l * jnp.exp(m - m_new) + jnp.sum(e, axis=0, keepdims=True)
        return m_new, l

    cols = heads * rows
    m0 = jnp.full((1, cols), -1e30, jnp.float32)
    l0 = jnp.zeros((1, cols), jnp.float32)
    m, l = lax.fori_loop(kb0, reach + 1, stat_step, (m0, l0))
    lse = m + jnp.log(l)

    def grad_step(c, carry):
        st, allowed = scores(c)
        p = jnp.where(allowed, jnp.exp(st - lse), 0.0)
        vc = kv_ref[c, :, width:]
        dpt = lax.dot_general(vc, doall[...], nt, preferred_element_type=jnp.float32)
        ds = (p * (dpt - delta)).astype(jnp.bfloat16)
        pb = p.astype(jnp.bfloat16)
        dk = jnp.dot(ds, qall[...], preferred_element_type=jnp.float32) * scaling
        dv = jnp.dot(pb, doall[...], preferred_element_type=jnp.float32)
        dkv_ref[c, :, :width] = dk
        dkv_ref[c, :, width:] = dv
        dqt[...] += jnp.dot(kt_ref[c], ds, preferred_element_type=jnp.float32)
        return carry

    lax.fori_loop(kb0, reach + 1, grad_step, 0)
    for h in range(heads):
        piece = dqt[:, h * rows:(h + 1) * rows]
        dq_ref[:, h * width:(h + 1) * width] = (piece.T * scaling).astype(jnp.bfloat16)


def body(queries, shared_keys, shared_values, outputs, out_grad, doc_lengths):
    rank = lax.axis_index("seq")
    n_seq = lax.axis_size("seq")
    rows = shared_keys.shape[0] // 2
    width = shared_keys.shape[1]
    heads = queries.shape[1] // width
    scaling = width ** (-0.5)
    win = REACH + 1
    doc_ends = jnp.cumsum(doc_lengths)
    doc_starts = doc_ends - doc_lengths
    blocks = jnp.stack([rank, 2 * n_seq - 1 - rank]).astype(jnp.int32)

    kv_local = jnp.concatenate([shared_keys, shared_values], axis=1)
    kv_all = lax.all_gather(kv_local, "seq", axis=0, tiled=True)
    kv_st = kv_all.reshape(n_seq, 2, rows, 2 * width)
    kv_seq = jnp.concatenate(
        [jnp.zeros((REACH, rows, 2 * width), kv_all.dtype), kv_st[:, 0], kv_st[::-1, 1]], axis=0
    )
    windows = jnp.stack(
        [lax.dynamic_slice_in_dim(kv_seq, blocks[i], win, 0) for i in range(2)]
    )
    kt = jnp.swapaxes(windows[..., :width], 2, 3)

    base_pos = jnp.arange(rows, dtype=jnp.int32)
    pos = blocks[:, None] * rows + base_pos[None, :]
    begins = jnp.max(
        jnp.where(doc_starts[None, None, :] <= pos[:, :, None], doc_starts[None, None, :], 0), axis=2
    ).astype(jnp.int32)
    kb0 = jnp.maximum(0, begins[:, 0] // rows - (blocks - REACH)).astype(jnp.int32)
    begin_t = jnp.tile(begins, (1, heads)).reshape(2, 1, heads * rows)
    qpos_t = jnp.tile(pos, (1, heads)).reshape(2, 1, heads * rows)
    prod = out_grad.astype(jnp.float32) * outputs.astype(jnp.float32)
    deltas = jnp.sum(prod.reshape(2, rows, heads, width), axis=3)
    delta_t = jnp.swapaxes(deltas, 1, 2).reshape(2, 1, heads * rows)

    kernel = functools.partial(
        _bwd_kernel, rows=rows, heads=heads, width=width, reach=REACH, scaling=scaling
    )
    cols = heads * rows
    grid_spec = pltpu.PrefetchScalarGridSpec(
        num_scalar_prefetch=2,
        grid=(2,),
        in_specs=[
            pl.BlockSpec((rows, cols), lambda s, blk, k0: (s, 0)),
            pl.BlockSpec((rows, cols), lambda s, blk, k0: (s, 0)),
            pl.BlockSpec((None, win, rows, 2 * width), lambda s, blk, k0: (s, 0, 0, 0)),
            pl.BlockSpec((None, win, width, rows), lambda s, blk, k0: (s, 0, 0, 0)),
            pl.BlockSpec((None, 1, cols), lambda s, blk, k0: (s, 0, 0)),
            pl.BlockSpec((None, 1, cols), lambda s, blk, k0: (s, 0, 0)),
            pl.BlockSpec((None, 1, cols), lambda s, blk, k0: (s, 0, 0)),
        ],
        out_specs=[
            pl.BlockSpec((rows, cols), lambda s, blk, k0: (s, 0)),
            pl.BlockSpec((None, win, rows, 2 * width), lambda s, blk, k0: (s, 0, 0, 0)),
        ],
        scratch_shapes=[
            pltpu.VMEM((cols, width), jnp.bfloat16),
            pltpu.VMEM((cols, width), jnp.bfloat16),
            pltpu.VMEM((width, cols), jnp.float32),
        ],
    )
    flops = 2 * 2 * win * 6 * rows * cols * width
    grad_queries, partial = pl.pallas_call(
        kernel,
        grid_spec=grid_spec,
        out_shape=[
            jax.ShapeDtypeStruct((2 * rows, cols), jnp.bfloat16),
            jax.ShapeDtypeStruct((2, win, rows, 2 * width), jnp.float32),
        ],
        compiler_params=pltpu.CompilerParams(dimension_semantics=("arbitrary",)),
        cost_estimate=pl.CostEstimate(
            flops=flops, transcendentals=2 * 2 * win * rows * cols, bytes_accessed=8 << 20
        ),
    )(blocks, kb0, queries, out_grad, windows, kt, begin_t, qpos_t, delta_t)

    acc = jnp.zeros((2 * n_seq + REACH, rows, 2 * width), jnp.float32)
    acc = lax.dynamic_update_slice_in_dim(acc, partial[0], blocks[0], 0)
    cur = lax.dynamic_slice_in_dim(acc, blocks[1], win, 0)
    acc = lax.dynamic_update_slice_in_dim(acc, cur + partial[1], blocks[1], 0)
    acc = acc[REACH:]
    storage = jnp.stack([acc[:n_seq], acc[n_seq:][::-1]], axis=1).reshape(2 * n_seq * rows, 2 * width)
    summed = lax.psum_scatter(storage, "seq", scatter_dimension=0, tiled=True)
    grad_keys = summed[:, :width].astype(jnp.bfloat16)
    grad_values = summed[:, width:].astype(jnp.bfloat16)
    return (grad_queries, grad_keys, grad_values)


def solution(mesh):
    placed = (
        P("seq", "grp"),
        P("seq", "grp"),
        P("seq", "grp"),
        P("seq", "grp"),
        P("seq", "grp"),
        P(),
    )
    return jax.shard_map(
        body,
        mesh=mesh,
        in_specs=placed,
        out_specs=(P("seq", "grp"), P("seq", "grp"), P("seq", "grp")),
        check_vma=False,
    )
```

```python
import functools

import jax
import jax.numpy as jnp
from jax import lax
from jax.experimental import pallas as pl
from jax.experimental.pallas import tpu as pltpu
from jax.sharding import PartitionSpec as P

REACH = 16


def _bwd_kernel(blk_ref, kb0_ref, q_ref, do_ref, kv_ref, kt_ref, begin_ref, qpos_ref,
                delta_ref, dq_ref, dkv_ref, qall, doall, dqt,
                *, rows, heads, width, reach, scaling):
    s = pl.program_id(0)
    b = blk_ref[s]
    kb0 = kb0_ref[s]
    for h in range(heads):
        qall[h * rows:(h + 1) * rows, :] = q_ref[:, h * width:(h + 1) * width]
        doall[h * rows:(h + 1) * rows, :] = do_ref[:, h * width:(h + 1) * width]
    begin = begin_ref[...]
    qpos = qpos_ref[...]
    delta = delta_ref[...]
    dqt[...] = jnp.zeros(dqt.shape, jnp.float32)
    dkv_ref[...] = jnp.zeros(dkv_ref.shape, jnp.float32)
    k_iota = lax.broadcasted_iota(jnp.int32, (rows, 1), 0)
    base = (b - reach) * rows
    nt = (((1,), (1,)), ((), ()))

    def scores(c):
        kc = kv_ref[c, :, :width]
        st = lax.dot_general(kc, qall[...], nt, preferred_element_type=jnp.float32) * scaling
        kpos = base + c * rows + k_iota
        allowed = (kpos >= begin) & (kpos <= qpos)
        return st, allowed

    def stat_step(c, carry):
        m, l = carry
        st, allowed = scores(c)
        masked = jnp.where(allowed, st, -1e30)
        m_new = jnp.maximum(m, jnp.max(masked, axis=0, keepdims=True))
        e = jnp.where(allowed, jnp.exp(st - m_new), 0.0)
        l = l * jnp.exp(m - m_new) + jnp.sum(e, axis=0, keepdims=True)
        return m_new, l

    cols = heads * rows
    m0 = jnp.full((1, cols), -1e30, jnp.float32)
    l0 = jnp.zeros((1, cols), jnp.float32)
    m, l = lax.fori_loop(kb0, reach + 1, stat_step, (m0, l0))
    lse = m + jnp.log(l)

    def grad_step(c, carry):
        st, allowed = scores(c)
        p = jnp.where(allowed, jnp.exp(st - lse), 0.0)
        vc = kv_ref[c, :, width:]
        dpt = lax.dot_general(vc, doall[...], nt, preferred_element_type=jnp.float32)
        ds = (p * (dpt - delta)).astype(jnp.bfloat16)
        pb = p.astype(jnp.bfloat16)
        dk = jnp.dot(ds, qall[...], preferred_element_type=jnp.float32) * scaling
        dv = jnp.dot(pb, doall[...], preferred_element_type=jnp.float32)
        dkv_ref[c, :, :width] = dk
        dkv_ref[c, :, width:] = dv
        dqt[...] += jnp.dot(kt_ref[c], ds, preferred_element_type=jnp.float32)
        return carry

    lax.fori_loop(kb0, reach + 1, grad_step, 0)
    for h in range(heads):
        piece = dqt[:, h * rows:(h + 1) * rows]
        dq_ref[:, h * width:(h + 1) * width] = (piece.T * scaling).astype(jnp.bfloat16)


def body(queries, shared_keys, shared_values, outputs, out_grad, doc_lengths):
    rank = lax.axis_index("seq")
    n_seq = lax.axis_size("seq")
    rows = shared_keys.shape[0] // 2
    width = shared_keys.shape[1]
    heads = queries.shape[1] // width
    scaling = width ** (-0.5)
    win = REACH + 1
    doc_ends = jnp.cumsum(doc_lengths)
    doc_starts = doc_ends - doc_lengths
    blocks = jnp.stack([rank, 2 * n_seq - 1 - rank]).astype(jnp.int32)

    kv_local = jnp.concatenate([shared_keys, shared_values], axis=1)
    kv_rep = jnp.broadcast_to(kv_local[None], (n_seq,) + kv_local.shape)
    kv_all = lax.all_to_all(kv_rep, "seq", 0, 0)
    kv_st = kv_all.reshape(n_seq, 2, rows, 2 * width)
    kv_seq = jnp.concatenate(
        [jnp.zeros((REACH, rows, 2 * width), kv_all.dtype), kv_st[:, 0], kv_st[::-1, 1]], axis=0
    )
    windows = jnp.stack(
        [lax.dynamic_slice_in_dim(kv_seq, blocks[i], win, 0) for i in range(2)]
    )
    kt = jnp.swapaxes(windows[..., :width], 2, 3)

    base_pos = jnp.arange(rows, dtype=jnp.int32)
    pos = blocks[:, None] * rows + base_pos[None, :]
    begins = jnp.max(
        jnp.where(doc_starts[None, None, :] <= pos[:, :, None], doc_starts[None, None, :], 0), axis=2
    ).astype(jnp.int32)
    kb0 = jnp.maximum(0, begins[:, 0] // rows - (blocks - REACH)).astype(jnp.int32)
    begin_t = jnp.tile(begins, (1, heads)).reshape(2, 1, heads * rows)
    qpos_t = jnp.tile(pos, (1, heads)).reshape(2, 1, heads * rows)
    prod = out_grad.astype(jnp.float32) * outputs.astype(jnp.float32)
    deltas = jnp.sum(prod.reshape(2, rows, heads, width), axis=3)
    delta_t = jnp.swapaxes(deltas, 1, 2).reshape(2, 1, heads * rows)

    kernel = functools.partial(
        _bwd_kernel, rows=rows, heads=heads, width=width, reach=REACH, scaling=scaling
    )
    cols = heads * rows
    grid_spec = pltpu.PrefetchScalarGridSpec(
        num_scalar_prefetch=2,
        grid=(2,),
        in_specs=[
            pl.BlockSpec((rows, cols), lambda s, blk, k0: (s, 0)),
            pl.BlockSpec((rows, cols), lambda s, blk, k0: (s, 0)),
            pl.BlockSpec((None, win, rows, 2 * width), lambda s, blk, k0: (s, 0, 0, 0)),
            pl.BlockSpec((None, win, width, rows), lambda s, blk, k0: (s, 0, 0, 0)),
            pl.BlockSpec((None, 1, cols), lambda s, blk, k0: (s, 0, 0)),
            pl.BlockSpec((None, 1, cols), lambda s, blk, k0: (s, 0, 0)),
            pl.BlockSpec((None, 1, cols), lambda s, blk, k0: (s, 0, 0)),
        ],
        out_specs=[
            pl.BlockSpec((rows, cols), lambda s, blk, k0: (s, 0)),
            pl.BlockSpec((None, win, rows, 2 * width), lambda s, blk, k0: (s, 0, 0, 0)),
        ],
        scratch_shapes=[
            pltpu.VMEM((cols, width), jnp.bfloat16),
            pltpu.VMEM((cols, width), jnp.bfloat16),
            pltpu.VMEM((width, cols), jnp.float32),
        ],
    )
    flops = 2 * 2 * win * 6 * rows * cols * width
    grad_queries, partial = pl.pallas_call(
        kernel,
        grid_spec=grid_spec,
        out_shape=[
            jax.ShapeDtypeStruct((2 * rows, cols), jnp.bfloat16),
            jax.ShapeDtypeStruct((2, win, rows, 2 * width), jnp.float32),
        ],
        compiler_params=pltpu.CompilerParams(dimension_semantics=("arbitrary",)),
        cost_estimate=pl.CostEstimate(
            flops=flops, transcendentals=2 * 2 * win * rows * cols, bytes_accessed=8 << 20
        ),
    )(blocks, kb0, queries, out_grad, windows, kt, begin_t, qpos_t, delta_t)

    acc = jnp.zeros((2 * n_seq + REACH, rows, 2 * width), jnp.float32)
    acc = lax.dynamic_update_slice_in_dim(acc, partial[0], blocks[0], 0)
    cur = lax.dynamic_slice_in_dim(acc, blocks[1], win, 0)
    acc = lax.dynamic_update_slice_in_dim(acc, cur + partial[1], blocks[1], 0)
    acc = acc[REACH:]
    storage = jnp.stack([acc[:n_seq], acc[n_seq:][::-1]], axis=1)
    received = lax.all_to_all(storage, "seq", 0, 0)
    summed = jnp.sum(received, axis=0).reshape(2 * rows, 2 * width)
    grad_keys = summed[:, :width].astype(jnp.bfloat16)
    grad_values = summed[:, width:].astype(jnp.bfloat16)
    return (grad_queries, grad_keys, grad_values)


def solution(mesh):
    placed = (
        P("seq", "grp"),
        P("seq", "grp"),
        P("seq", "grp"),
        P("seq", "grp"),
        P("seq", "grp"),
        P(),
    )
    return jax.shard_map(
        body,
        mesh=mesh,
        in_specs=placed,
        out_specs=(P("seq", "grp"), P("seq", "grp"), P("seq", "grp")),
        check_vma=False,
    )
```

```python
import functools

import jax
import jax.numpy as jnp
from jax import lax
from jax.experimental import pallas as pl
from jax.experimental.pallas import tpu as pltpu
from jax.sharding import PartitionSpec as P

REACH = 16


def _bwd_kernel(blk_ref, kb0_ref, q_ref, do_ref, kv_ref, kt_ref, begin_ref, qpos_ref,
                delta_ref, dq_ref, dkv_ref, qall, doall, dqt,
                *, rows, heads, width, reach, scaling):
    s = pl.program_id(0)
    b = blk_ref[s]
    kb0 = kb0_ref[s]
    for h in range(heads):
        qall[h * rows:(h + 1) * rows, :] = q_ref[:, h * width:(h + 1) * width]
        doall[h * rows:(h + 1) * rows, :] = do_ref[:, h * width:(h + 1) * width]
    begin = begin_ref[...]
    qpos = qpos_ref[...]
    delta = delta_ref[...]
    dqt[...] = jnp.zeros(dqt.shape, jnp.float32)
    dkv_ref[...] = jnp.zeros(dkv_ref.shape, jnp.float32)
    k_iota = lax.broadcasted_iota(jnp.int32, (rows, 1), 0)
    base = (b - reach) * rows
    nt = (((1,), (1,)), ((), ()))

    def scores(c):
        kc = kv_ref[c, :, :width]
        st = lax.dot_general(kc, qall[...], nt, preferred_element_type=jnp.float32) * scaling
        kpos = base + c * rows + k_iota
        allowed = (kpos >= begin) & (kpos <= qpos)
        return st, allowed

    def stat_step(c, carry):
        m, l = carry
        st, allowed = scores(c)
        masked = jnp.where(allowed, st, -1e30)
        m_new = jnp.maximum(m, jnp.max(masked, axis=0, keepdims=True))
        e = jnp.where(allowed, jnp.exp(st - m_new), 0.0)
        l = l * jnp.exp(m - m_new) + jnp.sum(e, axis=0, keepdims=True)
        return m_new, l

    cols = heads * rows
    m0 = jnp.full((1, cols), -1e30, jnp.float32)
    l0 = jnp.zeros((1, cols), jnp.float32)
    m, l = lax.fori_loop(kb0, reach + 1, stat_step, (m0, l0))
    lse = m + jnp.log(l)

    def grad_step(c, carry):
        st, allowed = scores(c)
        p = jnp.where(allowed, jnp.exp(st - lse), 0.0)
        vc = kv_ref[c, :, width:]
        dpt = lax.dot_general(vc, doall[...], nt, preferred_element_type=jnp.float32)
        ds = (p * (dpt - delta)).astype(jnp.bfloat16)
        pb = p.astype(jnp.bfloat16)
        dk = jnp.dot(ds, qall[...], preferred_element_type=jnp.float32) * scaling
        dv = jnp.dot(pb, doall[...], preferred_element_type=jnp.float32)
        dkv_ref[c, :, :width] = dk
        dkv_ref[c, :, width:] = dv
        dqt[...] += jnp.dot(kt_ref[c], ds, preferred_element_type=jnp.float32)
        return carry

    lax.fori_loop(kb0, reach + 1, grad_step, 0)
    for h in range(heads):
        piece = dqt[:, h * rows:(h + 1) * rows]
        dq_ref[:, h * width:(h + 1) * width] = (piece.T * scaling).astype(jnp.bfloat16)


def body(queries, shared_keys, shared_values, outputs, out_grad, doc_lengths):
    rank = lax.axis_index("seq")
    n_seq = lax.axis_size("seq")
    rows = shared_keys.shape[0] // 2
    width = shared_keys.shape[1]
    heads = queries.shape[1] // width
    scaling = width ** (-0.5)
    win = REACH + 1
    doc_ends = jnp.cumsum(doc_lengths)
    doc_starts = doc_ends - doc_lengths
    blocks = jnp.stack([rank, 2 * n_seq - 1 - rank]).astype(jnp.int32)

    kv_local = jnp.concatenate([shared_keys, shared_values], axis=1)
    kv_rep = jnp.broadcast_to(kv_local[None], (n_seq,) + kv_local.shape)
    kv_all = lax.all_to_all(kv_rep, "seq", 0, 0)
    kv_st = kv_all.reshape(n_seq, 2, rows, 2 * width)
    kv_seq = jnp.concatenate(
        [jnp.zeros((REACH, rows, 2 * width), kv_all.dtype), kv_st[:, 0], kv_st[::-1, 1]], axis=0
    )
    windows = jnp.stack(
        [lax.dynamic_slice_in_dim(kv_seq, blocks[i], win, 0) for i in range(2)]
    )
    kt = jnp.swapaxes(windows[..., :width], 2, 3)

    base_pos = jnp.arange(rows, dtype=jnp.int32)
    pos = blocks[:, None] * rows + base_pos[None, :]
    begins = jnp.max(
        jnp.where(doc_starts[None, None, :] <= pos[:, :, None], doc_starts[None, None, :], 0), axis=2
    ).astype(jnp.int32)
    kb0 = jnp.maximum(0, begins[:, 0] // rows - (blocks - REACH)).astype(jnp.int32)
    begin_t = jnp.tile(begins, (1, heads)).reshape(2, 1, heads * rows)
    qpos_t = jnp.tile(pos, (1, heads)).reshape(2, 1, heads * rows)
    prod = out_grad.astype(jnp.float32) * outputs.astype(jnp.float32)
    deltas = jnp.sum(prod.reshape(2, rows, heads, width), axis=3)
    delta_t = jnp.swapaxes(deltas, 1, 2).reshape(2, 1, heads * rows)

    kernel = functools.partial(
        _bwd_kernel, rows=rows, heads=heads, width=width, reach=REACH, scaling=scaling
    )
    cols = heads * rows
    grid_spec = pltpu.PrefetchScalarGridSpec(
        num_scalar_prefetch=2,
        grid=(2,),
        in_specs=[
            pl.BlockSpec((rows, cols), lambda s, blk, k0: (s, 0)),
            pl.BlockSpec((rows, cols), lambda s, blk, k0: (s, 0)),
            pl.BlockSpec((None, win, rows, 2 * width), lambda s, blk, k0: (s, 0, 0, 0)),
            pl.BlockSpec((None, win, width, rows), lambda s, blk, k0: (s, 0, 0, 0)),
            pl.BlockSpec((None, 1, cols), lambda s, blk, k0: (s, 0, 0)),
            pl.BlockSpec((None, 1, cols), lambda s, blk, k0: (s, 0, 0)),
            pl.BlockSpec((None, 1, cols), lambda s, blk, k0: (s, 0, 0)),
        ],
        out_specs=[
            pl.BlockSpec((rows, cols), lambda s, blk, k0: (s, 0)),
            pl.BlockSpec((None, win, rows, 2 * width), lambda s, blk, k0: (s, 0, 0, 0)),
        ],
        scratch_shapes=[
            pltpu.VMEM((cols, width), jnp.bfloat16),
            pltpu.VMEM((cols, width), jnp.bfloat16),
            pltpu.VMEM((width, cols), jnp.float32),
        ],
    )
    flops = 2 * 2 * win * 6 * rows * cols * width
    grad_queries, partial = pl.pallas_call(
        kernel,
        grid_spec=grid_spec,
        out_shape=[
            jax.ShapeDtypeStruct((2 * rows, cols), jnp.bfloat16),
            jax.ShapeDtypeStruct((2, win, rows, 2 * width), jnp.float32),
        ],
        compiler_params=pltpu.CompilerParams(dimension_semantics=("arbitrary",)),
        cost_estimate=pl.CostEstimate(
            flops=flops, transcendentals=2 * 2 * win * rows * cols, bytes_accessed=8 << 20
        ),
    )(blocks, kb0, queries, out_grad, windows, kt, begin_t, qpos_t, delta_t)

    acc = jnp.zeros((2 * n_seq + REACH, rows, 2 * width), jnp.float32)
    acc = lax.dynamic_update_slice_in_dim(acc, partial[0], blocks[0], 0)
    cur = lax.dynamic_slice_in_dim(acc, blocks[1], win, 0)
    acc = lax.dynamic_update_slice_in_dim(acc, cur + partial[1], blocks[1], 0)
    acc = acc[REACH:]
    storage = jnp.stack([acc[:n_seq], acc[n_seq:][::-1]], axis=1)
    received = lax.all_to_all(storage.astype(jnp.bfloat16), "seq", 0, 0)
    summed = jnp.sum(received.astype(jnp.float32), axis=0).reshape(2 * rows, 2 * width)
    grad_keys = summed[:, :width].astype(jnp.bfloat16)
    grad_values = summed[:, width:].astype(jnp.bfloat16)
    return (grad_queries, grad_keys, grad_values)


def solution(mesh):
    placed = (
        P("seq", "grp"),
        P("seq", "grp"),
        P("seq", "grp"),
        P("seq", "grp"),
        P("seq", "grp"),
        P(),
    )
    return jax.shard_map(
        body,
        mesh=mesh,
        in_specs=placed,
        out_specs=(P("seq", "grp"), P("seq", "grp"), P("seq", "grp")),
        check_vma=False,
    )
```

```python
import functools

import jax
import jax.numpy as jnp
from jax import lax
from jax.experimental import pallas as pl
from jax.experimental.pallas import tpu as pltpu
from jax.sharding import PartitionSpec as P

REACH = 16


def _bwd_kernel(blk_ref, kb0_ref, q_ref, do_ref, kv_ref, kt_ref, begin_ref, qpos_ref,
                delta_ref, dq_ref, dkv_ref, qall, doall, dqt,
                *, rows, heads, width, reach, scaling):
    s = pl.program_id(0)
    b = blk_ref[s]
    kb0 = kb0_ref[s]
    for h in range(heads):
        qall[h * rows:(h + 1) * rows, :] = q_ref[:, h * width:(h + 1) * width]
        doall[h * rows:(h + 1) * rows, :] = do_ref[:, h * width:(h + 1) * width]
    begin = begin_ref[...]
    qpos = qpos_ref[...]
    delta = delta_ref[...]
    dqt[...] = jnp.zeros(dqt.shape, jnp.float32)
    dkv_ref[...] = jnp.zeros(dkv_ref.shape, jnp.float32)
    k_iota = lax.broadcasted_iota(jnp.int32, (rows, 1), 0)
    base = (b - reach) * rows
    nt = (((1,), (1,)), ((), ()))

    def scores(c):
        kc = kv_ref[c, :, :width]
        st = lax.dot_general(kc, qall[...], nt, preferred_element_type=jnp.float32) * scaling
        kpos = base + c * rows + k_iota
        allowed = (kpos >= begin) & (kpos <= qpos)
        return st, allowed

    def stat_step(c, carry):
        m, l = carry
        st, allowed = scores(c)
        masked = jnp.where(allowed, st, -1e30)
        m_new = jnp.maximum(m, jnp.max(masked, axis=0, keepdims=True))
        e = jnp.where(allowed, jnp.exp(st - m_new), 0.0)
        l = l * jnp.exp(m - m_new) + jnp.sum(e, axis=0, keepdims=True)
        return m_new, l

    cols = heads * rows
    m0 = jnp.full((1, cols), -1e30, jnp.float32)
    l0 = jnp.zeros((1, cols), jnp.float32)
    m, l = lax.fori_loop(kb0, reach + 1, stat_step, (m0, l0))
    lse = m + jnp.log(l)

    def grad_step(c, carry):
        st, allowed = scores(c)
        p = jnp.where(allowed, jnp.exp(st - lse), 0.0)
        vc = kv_ref[c, :, width:]
        dpt = lax.dot_general(vc, doall[...], nt, preferred_element_type=jnp.float32)
        ds = (p * (dpt - delta)).astype(jnp.bfloat16)
        pb = p.astype(jnp.bfloat16)
        dk = jnp.dot(ds, qall[...], preferred_element_type=jnp.float32) * scaling
        dv = jnp.dot(pb, doall[...], preferred_element_type=jnp.float32)
        dkv_ref[c, :, :width] = dk
        dkv_ref[c, :, width:] = dv
        dqt[...] += jnp.dot(kt_ref[c], ds, preferred_element_type=jnp.float32)
        return carry

    lax.fori_loop(kb0, reach + 1, grad_step, 0)
    for h in range(heads):
        piece = dqt[:, h * rows:(h + 1) * rows]
        dq_ref[:, h * width:(h + 1) * width] = (piece.T * scaling).astype(jnp.bfloat16)


def body(queries, shared_keys, shared_values, outputs, out_grad, doc_lengths):
    n_in = lax.axis_size("w")
    rank = lax.axis_index("zp") * n_in + lax.axis_index("w")
    n_out = lax.axis_size("zp")
    n_seq = n_out * n_in
    rows = shared_keys.shape[0] // 2
    width = shared_keys.shape[1]
    heads = queries.shape[1] // width
    scaling = width ** (-0.5)
    win = REACH + 1
    doc_ends = jnp.cumsum(doc_lengths)
    doc_starts = doc_ends - doc_lengths
    blocks = jnp.stack([rank, 2 * n_seq - 1 - rank]).astype(jnp.int32)

    kv_local = jnp.concatenate([shared_keys, shared_values], axis=1)
    kv_col = lax.all_to_all(
        jnp.broadcast_to(kv_local[None], (n_out,) + kv_local.shape), "zp", 0, 0
    )
    kv_all = lax.all_to_all(
        jnp.broadcast_to(kv_col[None], (n_in,) + kv_col.shape), "w", 0, 0
    )
    kv_st = jnp.swapaxes(kv_all, 0, 1).reshape(n_seq, 2, rows, 2 * width)
    kv_seq = jnp.concatenate(
        [jnp.zeros((REACH, rows, 2 * width), kv_all.dtype), kv_st[:, 0], kv_st[::-1, 1]], axis=0
    )
    windows = jnp.stack(
        [lax.dynamic_slice_in_dim(kv_seq, blocks[i], win, 0) for i in range(2)]
    )
    kt = jnp.swapaxes(windows[..., :width], 2, 3)

    base_pos = jnp.arange(rows, dtype=jnp.int32)
    pos = blocks[:, None] * rows + base_pos[None, :]
    begins = jnp.max(
        jnp.where(doc_starts[None, None, :] <= pos[:, :, None], doc_starts[None, None, :], 0), axis=2
    ).astype(jnp.int32)
    kb0 = jnp.maximum(0, begins[:, 0] // rows - (blocks - REACH)).astype(jnp.int32)
    begin_t = jnp.tile(begins, (1, heads)).reshape(2, 1, heads * rows)
    qpos_t = jnp.tile(pos, (1, heads)).reshape(2, 1, heads * rows)
    prod = out_grad.astype(jnp.float32) * outputs.astype(jnp.float32)
    deltas = jnp.sum(prod.reshape(2, rows, heads, width), axis=3)
    delta_t = jnp.swapaxes(deltas, 1, 2).reshape(2, 1, heads * rows)

    kernel = functools.partial(
        _bwd_kernel, rows=rows, heads=heads, width=width, reach=REACH, scaling=scaling
    )
    cols = heads * rows
    grid_spec = pltpu.PrefetchScalarGridSpec(
        num_scalar_prefetch=2,
        grid=(2,),
        in_specs=[
            pl.BlockSpec((rows, cols), lambda s, blk, k0: (s, 0)),
            pl.BlockSpec((rows, cols), lambda s, blk, k0: (s, 0)),
            pl.BlockSpec((None, win, rows, 2 * width), lambda s, blk, k0: (s, 0, 0, 0)),
            pl.BlockSpec((None, win, width, rows), lambda s, blk, k0: (s, 0, 0, 0)),
            pl.BlockSpec((None, 1, cols), lambda s, blk, k0: (s, 0, 0)),
            pl.BlockSpec((None, 1, cols), lambda s, blk, k0: (s, 0, 0)),
            pl.BlockSpec((None, 1, cols), lambda s, blk, k0: (s, 0, 0)),
        ],
        out_specs=[
            pl.BlockSpec((rows, cols), lambda s, blk, k0: (s, 0)),
            pl.BlockSpec((None, win, rows, 2 * width), lambda s, blk, k0: (s, 0, 0, 0)),
        ],
        scratch_shapes=[
            pltpu.VMEM((cols, width), jnp.bfloat16),
            pltpu.VMEM((cols, width), jnp.bfloat16),
            pltpu.VMEM((width, cols), jnp.float32),
        ],
    )
    flops = 2 * 2 * win * 6 * rows * cols * width
    grad_queries, partial = pl.pallas_call(
        kernel,
        grid_spec=grid_spec,
        out_shape=[
            jax.ShapeDtypeStruct((2 * rows, cols), jnp.bfloat16),
            jax.ShapeDtypeStruct((2, win, rows, 2 * width), jnp.float32),
        ],
        compiler_params=pltpu.CompilerParams(dimension_semantics=("arbitrary",)),
        cost_estimate=pl.CostEstimate(
            flops=flops, transcendentals=2 * 2 * win * rows * cols, bytes_accessed=8 << 20
        ),
    )(blocks, kb0, queries, out_grad, windows, kt, begin_t, qpos_t, delta_t)

    acc = jnp.zeros((2 * n_seq + REACH, rows, 2 * width), jnp.float32)
    acc = lax.dynamic_update_slice_in_dim(acc, partial[0], blocks[0], 0)
    cur = lax.dynamic_slice_in_dim(acc, blocks[1], win, 0)
    acc = lax.dynamic_update_slice_in_dim(acc, cur + partial[1], blocks[1], 0)
    acc = acc[REACH:]
    storage = jnp.stack([acc[:n_seq], acc[n_seq:][::-1]], axis=1)
    storage = storage.reshape(n_out, n_in, 2, rows, 2 * width).astype(jnp.bfloat16)
    plane = lax.all_to_all(storage, "w", 1, 1)
    plane = jnp.sum(plane.astype(jnp.float32), axis=1)
    column = lax.all_to_all(plane, "zp", 0, 0)
    summed = jnp.sum(column, axis=0).reshape(2 * rows, 2 * width)
    grad_keys = summed[:, :width].astype(jnp.bfloat16)
    grad_values = summed[:, width:].astype(jnp.bfloat16)
    return (grad_queries, grad_keys, grad_values)


GROUP = 4


def solution(mesh):
    n_seq, n_grp = mesh.devices.shape
    split = mesh.devices.reshape(n_seq // GROUP, GROUP, n_grp)
    mesh2 = jax.sharding.Mesh(split, ("zp", "w", "grp"))
    rows = P(("zp", "w"), "grp")
    placed = (rows, rows, rows, rows, rows, P())
    return jax.shard_map(
        body,
        mesh=mesh2,
        in_specs=placed,
        out_specs=(rows, rows, rows),
        check_vma=False,
    )
```

```python
import functools

import jax
import jax.numpy as jnp
from jax import lax
from jax.experimental import pallas as pl
from jax.experimental.pallas import tpu as pltpu
from jax.sharding import PartitionSpec as P

REACH = 16


def _bwd_kernel(blk_ref, kb0_ref, q_ref, do_ref, kv_ref, kt_ref, begin_ref, qpos_ref,
                delta_ref, dq_ref, dkv_ref, qall, doall, dqt,
                *, rows, heads, width, reach, scaling):
    s = pl.program_id(0)
    b = blk_ref[s]
    kb0 = kb0_ref[s]
    for h in range(heads):
        qall[h * rows:(h + 1) * rows, :] = q_ref[:, h * width:(h + 1) * width]
        doall[h * rows:(h + 1) * rows, :] = do_ref[:, h * width:(h + 1) * width]
    begin = begin_ref[...]
    qpos = qpos_ref[...]
    delta = delta_ref[...]
    dqt[...] = jnp.zeros(dqt.shape, jnp.float32)
    dkv_ref[...] = jnp.zeros(dkv_ref.shape, jnp.float32)
    k_iota = lax.broadcasted_iota(jnp.int32, (rows, 1), 0)
    base = (b - reach) * rows
    nt = (((1,), (1,)), ((), ()))

    def scores(c):
        kc = kv_ref[c, :, :width]
        st = lax.dot_general(kc, qall[...], nt, preferred_element_type=jnp.float32) * scaling
        kpos = base + c * rows + k_iota
        allowed = (kpos >= begin) & (kpos <= qpos)
        return st, allowed

    def stat_step(c, carry):
        m, l = carry
        st, allowed = scores(c)
        masked = jnp.where(allowed, st, -1e30)
        m_new = jnp.maximum(m, jnp.max(masked, axis=0, keepdims=True))
        e = jnp.where(allowed, jnp.exp(st - m_new), 0.0)
        l = l * jnp.exp(m - m_new) + jnp.sum(e, axis=0, keepdims=True)
        return m_new, l

    cols = heads * rows
    m0 = jnp.full((1, cols), -1e30, jnp.float32)
    l0 = jnp.zeros((1, cols), jnp.float32)
    m, l = lax.fori_loop(kb0, reach + 1, stat_step, (m0, l0))
    lse = m + jnp.log(l)

    def grad_step(c, carry):
        st, allowed = scores(c)
        p = jnp.where(allowed, jnp.exp(st - lse), 0.0)
        vc = kv_ref[c, :, width:]
        dpt = lax.dot_general(vc, doall[...], nt, preferred_element_type=jnp.float32)
        ds = (p * (dpt - delta)).astype(jnp.bfloat16)
        pb = p.astype(jnp.bfloat16)
        dk = jnp.dot(ds, qall[...], preferred_element_type=jnp.float32) * scaling
        dv = jnp.dot(pb, doall[...], preferred_element_type=jnp.float32)
        dkv_ref[c, :, :width] = dk
        dkv_ref[c, :, width:] = dv
        dqt[...] += jnp.dot(kt_ref[c], ds, preferred_element_type=jnp.float32)
        return carry

    lax.fori_loop(kb0, reach + 1, grad_step, 0)
    for h in range(heads):
        piece = dqt[:, h * rows:(h + 1) * rows]
        dq_ref[:, h * width:(h + 1) * width] = (piece.T * scaling).astype(jnp.bfloat16)


def body(queries, shared_keys, shared_values, outputs, out_grad, doc_lengths):
    n_in = lax.axis_size("w")
    rank = lax.axis_index("zp") * n_in + lax.axis_index("w")
    n_out = lax.axis_size("zp")
    n_seq = n_out * n_in
    rows = shared_keys.shape[0] // 2
    width = shared_keys.shape[1]
    heads = queries.shape[1] // width
    scaling = width ** (-0.5)
    win = REACH + 1
    doc_ends = jnp.cumsum(doc_lengths)
    doc_starts = doc_ends - doc_lengths
    blocks = jnp.stack([rank, 2 * n_seq - 1 - rank]).astype(jnp.int32)

    kv_local = jnp.concatenate([shared_keys, shared_values], axis=1)
    kv_col = lax.all_to_all(
        jnp.broadcast_to(kv_local[None], (n_out,) + kv_local.shape), "zp", 0, 0
    )
    kv_all = lax.all_to_all(
        jnp.broadcast_to(kv_col[None], (n_in,) + kv_col.shape), "w", 0, 0
    )
    kv_st = jnp.swapaxes(kv_all, 0, 1).reshape(n_seq, 2, rows, 2 * width)
    kv_seq = jnp.concatenate(
        [jnp.zeros((REACH, rows, 2 * width), kv_all.dtype), kv_st[:, 0], kv_st[::-1, 1]], axis=0
    )
    windows = jnp.stack(
        [lax.dynamic_slice_in_dim(kv_seq, blocks[i], win, 0) for i in range(2)]
    )
    kt = jnp.swapaxes(windows[..., :width], 2, 3)

    base_pos = jnp.arange(rows, dtype=jnp.int32)
    pos = blocks[:, None] * rows + base_pos[None, :]
    begins = jnp.max(
        jnp.where(doc_starts[None, None, :] <= pos[:, :, None], doc_starts[None, None, :], 0), axis=2
    ).astype(jnp.int32)
    kb0 = jnp.maximum(0, begins[:, 0] // rows - (blocks - REACH)).astype(jnp.int32)
    begin_t = jnp.tile(begins, (1, heads)).reshape(2, 1, heads * rows)
    qpos_t = jnp.tile(pos, (1, heads)).reshape(2, 1, heads * rows)
    prod = out_grad.astype(jnp.float32) * outputs.astype(jnp.float32)
    deltas = jnp.sum(prod.reshape(2, rows, heads, width), axis=3)
    delta_t = jnp.swapaxes(deltas, 1, 2).reshape(2, 1, heads * rows)

    kernel = functools.partial(
        _bwd_kernel, rows=rows, heads=heads, width=width, reach=REACH, scaling=scaling
    )
    cols = heads * rows
    grid_spec = pltpu.PrefetchScalarGridSpec(
        num_scalar_prefetch=2,
        grid=(2,),
        in_specs=[
            pl.BlockSpec((rows, cols), lambda s, blk, k0: (s, 0)),
            pl.BlockSpec((rows, cols), lambda s, blk, k0: (s, 0)),
            pl.BlockSpec((None, win, rows, 2 * width), lambda s, blk, k0: (s, 0, 0, 0)),
            pl.BlockSpec((None, win, width, rows), lambda s, blk, k0: (s, 0, 0, 0)),
            pl.BlockSpec((None, 1, cols), lambda s, blk, k0: (s, 0, 0)),
            pl.BlockSpec((None, 1, cols), lambda s, blk, k0: (s, 0, 0)),
            pl.BlockSpec((None, 1, cols), lambda s, blk, k0: (s, 0, 0)),
        ],
        out_specs=[
            pl.BlockSpec((rows, cols), lambda s, blk, k0: (s, 0)),
            pl.BlockSpec((None, win, rows, 2 * width), lambda s, blk, k0: (s, 0, 0, 0)),
        ],
        scratch_shapes=[
            pltpu.VMEM((cols, width), jnp.bfloat16),
            pltpu.VMEM((cols, width), jnp.bfloat16),
            pltpu.VMEM((width, cols), jnp.float32),
        ],
    )
    flops = 2 * 2 * win * 6 * rows * cols * width
    grad_queries, partial = pl.pallas_call(
        kernel,
        grid_spec=grid_spec,
        out_shape=[
            jax.ShapeDtypeStruct((2 * rows, cols), jnp.bfloat16),
            jax.ShapeDtypeStruct((2, win, rows, 2 * width), jnp.float32),
        ],
        compiler_params=pltpu.CompilerParams(dimension_semantics=("arbitrary",)),
        cost_estimate=pl.CostEstimate(
            flops=flops, transcendentals=2 * 2 * win * rows * cols, bytes_accessed=8 << 20
        ),
    )(blocks, kb0, queries, out_grad, windows, kt, begin_t, qpos_t, delta_t)

    acc = jnp.zeros((2 * n_seq + REACH, rows, 2 * width), jnp.float32)
    acc = lax.dynamic_update_slice_in_dim(acc, partial[0], blocks[0], 0)
    cur = lax.dynamic_slice_in_dim(acc, blocks[1], win, 0)
    acc = lax.dynamic_update_slice_in_dim(acc, cur + partial[1], blocks[1], 0)
    acc = acc[REACH:]
    storage = jnp.stack([acc[:n_seq], acc[n_seq:][::-1]], axis=1)
    storage = storage.reshape(n_out, n_in, 2, rows, 2 * width).astype(jnp.bfloat16)
    plane = lax.all_to_all(storage, "w", 1, 1)
    plane = jnp.sum(plane.astype(jnp.float32), axis=1)
    column = lax.all_to_all(plane.astype(jnp.bfloat16), "zp", 0, 0)
    summed = jnp.sum(column.astype(jnp.float32), axis=0).reshape(2 * rows, 2 * width)
    grad_keys = summed[:, :width].astype(jnp.bfloat16)
    grad_values = summed[:, width:].astype(jnp.bfloat16)
    return (grad_queries, grad_keys, grad_values)


GROUP = 4


def solution(mesh):
    n_seq, n_grp = mesh.devices.shape
    split = mesh.devices.reshape(n_seq // GROUP, GROUP, n_grp)
    mesh2 = jax.sharding.Mesh(split, ("zp", "w", "grp"))
    rows = P(("zp", "w"), "grp")
    placed = (rows, rows, rows, rows, rows, P())
    return jax.shard_map(
        body,
        mesh=mesh2,
        in_specs=placed,
        out_specs=(rows, rows, rows),
        check_vma=False,
    )
```

```python
import functools

import jax
import jax.numpy as jnp
from jax import lax
from jax.experimental import pallas as pl
from jax.experimental.pallas import tpu as pltpu
from jax.sharding import PartitionSpec as P

REACH = 16


def _bwd_kernel(blk_ref, kb0_ref, q_ref, do_ref, kv_ref, kt_ref, begin_ref, qpos_ref,
                delta_ref, dq_ref, dkv_ref, qall, doall, dqt,
                *, rows, heads, width, reach, scaling):
    s = pl.program_id(0)
    b = blk_ref[s]
    kb0 = kb0_ref[s]
    for h in range(heads):
        qall[h * rows:(h + 1) * rows, :] = q_ref[:, h * width:(h + 1) * width]
        doall[h * rows:(h + 1) * rows, :] = do_ref[:, h * width:(h + 1) * width]
    begin = begin_ref[...]
    qpos = qpos_ref[...]
    delta = delta_ref[...]
    dqt[...] = jnp.zeros(dqt.shape, jnp.float32)
    dkv_ref[...] = jnp.zeros(dkv_ref.shape, jnp.float32)
    k_iota = lax.broadcasted_iota(jnp.int32, (rows, 1), 0)
    base = (b - reach) * rows
    nt = (((1,), (1,)), ((), ()))

    def scores(c):
        kc = kv_ref[c, :, :width]
        st = lax.dot_general(kc, qall[...], nt, preferred_element_type=jnp.float32) * scaling
        kpos = base + c * rows + k_iota
        allowed = (kpos >= begin) & (kpos <= qpos)
        return st, allowed

    def stat_step(c, carry):
        m, l = carry
        st, allowed = scores(c)
        masked = jnp.where(allowed, st, -1e30)
        m_new = jnp.maximum(m, jnp.max(masked, axis=0, keepdims=True))
        e = jnp.where(allowed, jnp.exp(st - m_new), 0.0)
        l = l * jnp.exp(m - m_new) + jnp.sum(e, axis=0, keepdims=True)
        return m_new, l

    cols = heads * rows
    m0 = jnp.full((1, cols), -1e30, jnp.float32)
    l0 = jnp.zeros((1, cols), jnp.float32)
    m, l = lax.fori_loop(kb0, reach + 1, stat_step, (m0, l0))
    lse = m + jnp.log(l)

    def grad_step(c, carry):
        st, allowed = scores(c)
        p = jnp.where(allowed, jnp.exp(st - lse), 0.0)
        vc = kv_ref[c, :, width:]
        dpt = lax.dot_general(vc, doall[...], nt, preferred_element_type=jnp.float32)
        ds = (p * (dpt - delta)).astype(jnp.bfloat16)
        pb = p.astype(jnp.bfloat16)
        dk = jnp.dot(ds, qall[...], preferred_element_type=jnp.float32) * scaling
        dv = jnp.dot(pb, doall[...], preferred_element_type=jnp.float32)
        dkv_ref[c, :, :width] = dk
        dkv_ref[c, :, width:] = dv
        dqt[...] += jnp.dot(kt_ref[c], ds, preferred_element_type=jnp.float32)
        return carry

    lax.fori_loop(kb0, reach + 1, grad_step, 0)
    for h in range(heads):
        piece = dqt[:, h * rows:(h + 1) * rows]
        dq_ref[:, h * width:(h + 1) * width] = (piece.T * scaling).astype(jnp.bfloat16)


def _shift(x, k, n):
    return lax.ppermute(x, "zp", [(i, (i + k) % n) for i in range(n)])


def _column_gather(x, n):
    me = lax.axis_index("zp")
    got = jnp.stack([x] + [_shift(x, k, n) for k in range(1, n)])
    order = (me - jnp.arange(n)) % n
    return jnp.take(got, order, axis=0)


def _column_reduce(plane, n):
    me = lax.axis_index("zp")
    total = lax.dynamic_index_in_dim(plane, me, 0, keepdims=False)
    for k in range(1, n):
        piece = lax.dynamic_index_in_dim(plane, (me + k) % n, 0, keepdims=False)
        total = total + _shift(piece.astype(jnp.bfloat16), k, n).astype(jnp.float32)
    return total


def body(queries, shared_keys, shared_values, outputs, out_grad, doc_lengths):
    n_in = lax.axis_size("w")
    rank = lax.axis_index("zp") * n_in + lax.axis_index("w")
    n_out = lax.axis_size("zp")
    n_seq = n_out * n_in
    rows = shared_keys.shape[0] // 2
    width = shared_keys.shape[1]
    heads = queries.shape[1] // width
    scaling = width ** (-0.5)
    win = REACH + 1
    doc_ends = jnp.cumsum(doc_lengths)
    doc_starts = doc_ends - doc_lengths
    blocks = jnp.stack([rank, 2 * n_seq - 1 - rank]).astype(jnp.int32)

    kv_local = jnp.concatenate([shared_keys, shared_values], axis=1)
    kv_col = _column_gather(kv_local, n_out)
    kv_all = lax.all_to_all(
        jnp.broadcast_to(kv_col[None], (n_in,) + kv_col.shape), "w", 0, 0
    )
    kv_st = jnp.swapaxes(kv_all, 0, 1).reshape(n_seq, 2, rows, 2 * width)
    kv_seq = jnp.concatenate(
        [jnp.zeros((REACH, rows, 2 * width), kv_all.dtype), kv_st[:, 0], kv_st[::-1, 1]], axis=0
    )
    windows = jnp.stack(
        [lax.dynamic_slice_in_dim(kv_seq, blocks[i], win, 0) for i in range(2)]
    )
    kt = jnp.swapaxes(windows[..., :width], 2, 3)

    base_pos = jnp.arange(rows, dtype=jnp.int32)
    pos = blocks[:, None] * rows + base_pos[None, :]
    begins = jnp.max(
        jnp.where(doc_starts[None, None, :] <= pos[:, :, None], doc_starts[None, None, :], 0), axis=2
    ).astype(jnp.int32)
    kb0 = jnp.maximum(0, begins[:, 0] // rows - (blocks - REACH)).astype(jnp.int32)
    begin_t = jnp.tile(begins, (1, heads)).reshape(2, 1, heads * rows)
    qpos_t = jnp.tile(pos, (1, heads)).reshape(2, 1, heads * rows)
    prod = out_grad.astype(jnp.float32) * outputs.astype(jnp.float32)
    deltas = jnp.sum(prod.reshape(2, rows, heads, width), axis=3)
    delta_t = jnp.swapaxes(deltas, 1, 2).reshape(2, 1, heads * rows)

    kernel = functools.partial(
        _bwd_kernel, rows=rows, heads=heads, width=width, reach=REACH, scaling=scaling
    )
    cols = heads * rows
    grid_spec = pltpu.PrefetchScalarGridSpec(
        num_scalar_prefetch=2,
        grid=(2,),
        in_specs=[
            pl.BlockSpec((rows, cols), lambda s, blk, k0: (s, 0)),
            pl.BlockSpec((rows, cols), lambda s, blk, k0: (s, 0)),
            pl.BlockSpec((None, win, rows, 2 * width), lambda s, blk, k0: (s, 0, 0, 0)),
            pl.BlockSpec((None, win, width, rows), lambda s, blk, k0: (s, 0, 0, 0)),
            pl.BlockSpec((None, 1, cols), lambda s, blk, k0: (s, 0, 0)),
            pl.BlockSpec((None, 1, cols), lambda s, blk, k0: (s, 0, 0)),
            pl.BlockSpec((None, 1, cols), lambda s, blk, k0: (s, 0, 0)),
        ],
        out_specs=[
            pl.BlockSpec((rows, cols), lambda s, blk, k0: (s, 0)),
            pl.BlockSpec((None, win, rows, 2 * width), lambda s, blk, k0: (s, 0, 0, 0)),
        ],
        scratch_shapes=[
            pltpu.VMEM((cols, width), jnp.bfloat16),
            pltpu.VMEM((cols, width), jnp.bfloat16),
            pltpu.VMEM((width, cols), jnp.float32),
        ],
    )
    flops = 2 * 2 * win * 6 * rows * cols * width
    grad_queries, partial = pl.pallas_call(
        kernel,
        grid_spec=grid_spec,
        out_shape=[
            jax.ShapeDtypeStruct((2 * rows, cols), jnp.bfloat16),
            jax.ShapeDtypeStruct((2, win, rows, 2 * width), jnp.float32),
        ],
        compiler_params=pltpu.CompilerParams(dimension_semantics=("arbitrary",)),
        cost_estimate=pl.CostEstimate(
            flops=flops, transcendentals=2 * 2 * win * rows * cols, bytes_accessed=8 << 20
        ),
    )(blocks, kb0, queries, out_grad, windows, kt, begin_t, qpos_t, delta_t)

    acc = jnp.zeros((2 * n_seq + REACH, rows, 2 * width), jnp.float32)
    acc = lax.dynamic_update_slice_in_dim(acc, partial[0], blocks[0], 0)
    cur = lax.dynamic_slice_in_dim(acc, blocks[1], win, 0)
    acc = lax.dynamic_update_slice_in_dim(acc, cur + partial[1], blocks[1], 0)
    acc = acc[REACH:]
    storage = jnp.stack([acc[:n_seq], acc[n_seq:][::-1]], axis=1)
    storage = storage.reshape(n_out, n_in, 2, rows, 2 * width).astype(jnp.bfloat16)
    plane = lax.all_to_all(storage, "w", 1, 1)
    plane = jnp.sum(plane.astype(jnp.float32), axis=1)
    summed = _column_reduce(plane, n_out).reshape(2 * rows, 2 * width)
    grad_keys = summed[:, :width].astype(jnp.bfloat16)
    grad_values = summed[:, width:].astype(jnp.bfloat16)
    return (grad_queries, grad_keys, grad_values)


GROUP = 4


def solution(mesh):
    n_seq, n_grp = mesh.devices.shape
    split = mesh.devices.reshape(n_seq // GROUP, GROUP, n_grp)
    mesh2 = jax.sharding.Mesh(split, ("zp", "w", "grp"))
    rows = P(("zp", "w"), "grp")
    placed = (rows, rows, rows, rows, rows, P())
    return jax.shard_map(
        body,
        mesh=mesh2,
        in_specs=placed,
        out_specs=(rows, rows, rows),
        check_vma=False,
    )
```

```python
import functools

import jax
import jax.numpy as jnp
from jax import lax
from jax.experimental import pallas as pl
from jax.experimental.pallas import tpu as pltpu
from jax.sharding import PartitionSpec as P

REACH = 16


def _bwd_kernel(blk_ref, kb0_ref, q_ref, do_ref, kv_ref, kt_ref, begin_ref, qpos_ref,
                delta_ref, dq_ref, dkv_ref, qall, doall, dqt,
                *, rows, heads, width, reach, scaling):
    s = pl.program_id(0)
    b = blk_ref[s]
    kb0 = kb0_ref[s]
    for h in range(heads):
        qall[h * rows:(h + 1) * rows, :] = q_ref[:, h * width:(h + 1) * width]
        doall[h * rows:(h + 1) * rows, :] = do_ref[:, h * width:(h + 1) * width]
    begin = begin_ref[...]
    qpos = qpos_ref[...]
    delta = delta_ref[...]
    dqt[...] = jnp.zeros(dqt.shape, jnp.float32)
    dkv_ref[...] = jnp.zeros(dkv_ref.shape, jnp.float32)
    k_iota = lax.broadcasted_iota(jnp.int32, (rows, 1), 0)
    base = (b - reach) * rows
    nt = (((1,), (1,)), ((), ()))

    def scores(c):
        kc = kv_ref[c, :, :width]
        st = lax.dot_general(kc, qall[...], nt, preferred_element_type=jnp.float32) * scaling
        kpos = base + c * rows + k_iota
        allowed = (kpos >= begin) & (kpos <= qpos)
        return st, allowed

    def stat_step(c, carry):
        m, l = carry
        st, allowed = scores(c)
        masked = jnp.where(allowed, st, -1e30)
        m_new = jnp.maximum(m, jnp.max(masked, axis=0, keepdims=True))
        e = jnp.where(allowed, jnp.exp(st - m_new), 0.0)
        l = l * jnp.exp(m - m_new) + jnp.sum(e, axis=0, keepdims=True)
        return m_new, l

    cols = heads * rows
    m0 = jnp.full((1, cols), -1e30, jnp.float32)
    l0 = jnp.zeros((1, cols), jnp.float32)
    m, l = lax.fori_loop(kb0, reach + 1, stat_step, (m0, l0))
    lse = m + jnp.log(l)

    def grad_step(c, carry):
        st, allowed = scores(c)
        p = jnp.where(allowed, jnp.exp(st - lse), 0.0)
        vc = kv_ref[c, :, width:]
        dpt = lax.dot_general(vc, doall[...], nt, preferred_element_type=jnp.float32)
        ds = (p * (dpt - delta)).astype(jnp.bfloat16)
        pb = p.astype(jnp.bfloat16)
        dk = jnp.dot(ds, qall[...], preferred_element_type=jnp.float32) * scaling
        dv = jnp.dot(pb, doall[...], preferred_element_type=jnp.float32)
        dkv_ref[c, :, :width] = dk
        dkv_ref[c, :, width:] = dv
        dqt[...] += jnp.dot(kt_ref[c], ds, preferred_element_type=jnp.float32)
        return carry

    lax.fori_loop(kb0, reach + 1, grad_step, 0)
    for h in range(heads):
        piece = dqt[:, h * rows:(h + 1) * rows]
        dq_ref[:, h * width:(h + 1) * width] = (piece.T * scaling).astype(jnp.bfloat16)


def _shift(x, k, n, axis):
    return lax.ppermute(x, axis, [(i, (i + k) % n) for i in range(n)])


def _group_gather(x, n, axis):
    me = lax.axis_index(axis)
    got = jnp.stack([x] + [_shift(x, k, n, axis) for k in range(1, n)])
    order = (me - jnp.arange(n)) % n
    return jnp.take(got, order, axis=0)


def _group_reduce(parts, n, axis, dim):
    me = lax.axis_index(axis)
    total = lax.dynamic_index_in_dim(parts, me, dim, keepdims=False).astype(jnp.float32)
    for k in range(1, n):
        piece = lax.dynamic_index_in_dim(parts, (me + k) % n, dim, keepdims=False)
        total = total + _shift(piece.astype(jnp.bfloat16), k, n, axis).astype(jnp.float32)
    return total


def body(queries, shared_keys, shared_values, outputs, out_grad, doc_lengths):
    n_in = lax.axis_size("w")
    rank = lax.axis_index("zp") * n_in + lax.axis_index("w")
    n_out = lax.axis_size("zp")
    n_seq = n_out * n_in
    rows = shared_keys.shape[0] // 2
    width = shared_keys.shape[1]
    heads = queries.shape[1] // width
    scaling = width ** (-0.5)
    win = REACH + 1
    doc_ends = jnp.cumsum(doc_lengths)
    doc_starts = doc_ends - doc_lengths
    blocks = jnp.stack([rank, 2 * n_seq - 1 - rank]).astype(jnp.int32)

    kv_local = jnp.concatenate([shared_keys, shared_values], axis=1)
    kv_col = _group_gather(kv_local, n_out, "zp")
    kv_all = _group_gather(kv_col, n_in, "w")
    kv_st = jnp.swapaxes(kv_all, 0, 1).reshape(n_seq, 2, rows, 2 * width)
    kv_seq = jnp.concatenate(
        [jnp.zeros((REACH, rows, 2 * width), kv_all.dtype), kv_st[:, 0], kv_st[::-1, 1]], axis=0
    )
    windows = jnp.stack(
        [lax.dynamic_slice_in_dim(kv_seq, blocks[i], win, 0) for i in range(2)]
    )
    kt = jnp.swapaxes(windows[..., :width], 2, 3)

    base_pos = jnp.arange(rows, dtype=jnp.int32)
    pos = blocks[:, None] * rows + base_pos[None, :]
    begins = jnp.max(
        jnp.where(doc_starts[None, None, :] <= pos[:, :, None], doc_starts[None, None, :], 0), axis=2
    ).astype(jnp.int32)
    kb0 = jnp.maximum(0, begins[:, 0] // rows - (blocks - REACH)).astype(jnp.int32)
    begin_t = jnp.tile(begins, (1, heads)).reshape(2, 1, heads * rows)
    qpos_t = jnp.tile(pos, (1, heads)).reshape(2, 1, heads * rows)
    prod = out_grad.astype(jnp.float32) * outputs.astype(jnp.float32)
    deltas = jnp.sum(prod.reshape(2, rows, heads, width), axis=3)
    delta_t = jnp.swapaxes(deltas, 1, 2).reshape(2, 1, heads * rows)

    kernel = functools.partial(
        _bwd_kernel, rows=rows, heads=heads, width=width, reach=REACH, scaling=scaling
    )
    cols = heads * rows
    grid_spec = pltpu.PrefetchScalarGridSpec(
        num_scalar_prefetch=2,
        grid=(2,),
        in_specs=[
            pl.BlockSpec((rows, cols), lambda s, blk, k0: (s, 0)),
            pl.BlockSpec((rows, cols), lambda s, blk, k0: (s, 0)),
            pl.BlockSpec((None, win, rows, 2 * width), lambda s, blk, k0: (s, 0, 0, 0)),
            pl.BlockSpec((None, win, width, rows), lambda s, blk, k0: (s, 0, 0, 0)),
            pl.BlockSpec((None, 1, cols), lambda s, blk, k0: (s, 0, 0)),
            pl.BlockSpec((None, 1, cols), lambda s, blk, k0: (s, 0, 0)),
            pl.BlockSpec((None, 1, cols), lambda s, blk, k0: (s, 0, 0)),
        ],
        out_specs=[
            pl.BlockSpec((rows, cols), lambda s, blk, k0: (s, 0)),
            pl.BlockSpec((None, win, rows, 2 * width), lambda s, blk, k0: (s, 0, 0, 0)),
        ],
        scratch_shapes=[
            pltpu.VMEM((cols, width), jnp.bfloat16),
            pltpu.VMEM((cols, width), jnp.bfloat16),
            pltpu.VMEM((width, cols), jnp.float32),
        ],
    )
    flops = 2 * 2 * win * 6 * rows * cols * width
    grad_queries, partial = pl.pallas_call(
        kernel,
        grid_spec=grid_spec,
        out_shape=[
            jax.ShapeDtypeStruct((2 * rows, cols), jnp.bfloat16),
            jax.ShapeDtypeStruct((2, win, rows, 2 * width), jnp.float32),
        ],
        compiler_params=pltpu.CompilerParams(dimension_semantics=("arbitrary",)),
        cost_estimate=pl.CostEstimate(
            flops=flops, transcendentals=2 * 2 * win * rows * cols, bytes_accessed=8 << 20
        ),
    )(blocks, kb0, queries, out_grad, windows, kt, begin_t, qpos_t, delta_t)

    acc = jnp.zeros((2 * n_seq + REACH, rows, 2 * width), jnp.float32)
    acc = lax.dynamic_update_slice_in_dim(acc, partial[0], blocks[0], 0)
    cur = lax.dynamic_slice_in_dim(acc, blocks[1], win, 0)
    acc = lax.dynamic_update_slice_in_dim(acc, cur + partial[1], blocks[1], 0)
    acc = acc[REACH:]
    storage = jnp.stack([acc[:n_seq], acc[n_seq:][::-1]], axis=1)
    storage = storage.reshape(n_out, n_in, 2, rows, 2 * width).astype(jnp.bfloat16)
    plane = _group_reduce(storage, n_in, "w", 1)
    summed = _group_reduce(plane, n_out, "zp", 0).reshape(2 * rows, 2 * width)
    grad_keys = summed[:, :width].astype(jnp.bfloat16)
    grad_values = summed[:, width:].astype(jnp.bfloat16)
    return (grad_queries, grad_keys, grad_values)


GROUP = 4


def solution(mesh):
    n_seq, n_grp = mesh.devices.shape
    split = mesh.devices.reshape(n_seq // GROUP, GROUP, n_grp)
    mesh2 = jax.sharding.Mesh(split, ("zp", "w", "grp"))
    rows = P(("zp", "w"), "grp")
    placed = (rows, rows, rows, rows, rows, P())
    return jax.shard_map(
        body,
        mesh=mesh2,
        in_specs=placed,
        out_specs=(rows, rows, rows),
        check_vma=False,
    )
```

```python
import functools

import jax
import jax.numpy as jnp
from jax import lax
from jax.experimental import pallas as pl
from jax.experimental.pallas import tpu as pltpu
from jax.sharding import PartitionSpec as P

REACH = 16


def _bwd_kernel(blk_ref, kb0_ref, srow_ref, dst_ref, q_ref, do_ref, kv_hbm, begin_ref,
                qpos_ref, delta_ref, dq_ref, part_ref, qall, doall, dqt, kvbuf, sems,
                *, rows, heads, width, reach, scaling):
    s = pl.program_id(0)
    win = reach + 1

    def copy(side, i):
        row = pl.multiple_of(srow_ref[side * win + i], rows)
        return pltpu.make_async_copy(
            kv_hbm.at[pl.ds(row, rows)], kvbuf.at[side, i], sems.at[side, i]
        )

    @pl.when(s == 0)
    def _():
        for side in range(2):
            for i in range(win):
                copy(side, i).start()
        part_ref[...] = jnp.zeros(part_ref.shape, jnp.float32)

    b = blk_ref[s]
    kb0 = kb0_ref[s]
    for h in range(heads):
        qall[h * rows:(h + 1) * rows, :] = q_ref[:, h * width:(h + 1) * width]
        doall[h * rows:(h + 1) * rows, :] = do_ref[:, h * width:(h + 1) * width]
    begin = begin_ref[...]
    qpos = qpos_ref[...]
    delta = delta_ref[...]
    dqt[...] = jnp.zeros(dqt.shape, jnp.float32)
    k_iota = lax.broadcasted_iota(jnp.int32, (rows, 1), 0)
    base = (b - reach) * rows
    nt = (((1,), (1,)), ((), ()))
    tn = (((0,), (0,)), ((), ()))
    for i in range(win):
        copy(s, i).wait()

    def scores(c):
        kc = kvbuf[s, c, :, :width]
        st = lax.dot_general(kc, qall[...], nt, preferred_element_type=jnp.float32) * scaling
        kpos = base + c * rows + k_iota
        allowed = (kpos >= begin) & (kpos <= qpos)
        return kc, st, allowed

    def stat_step(c, carry):
        m, l = carry
        _, st, allowed = scores(c)
        masked = jnp.where(allowed, st, -1e30)
        m_new = jnp.maximum(m, jnp.max(masked, axis=0, keepdims=True))
        e = jnp.where(allowed, jnp.exp(st - m_new), 0.0)
        l = l * jnp.exp(m - m_new) + jnp.sum(e, axis=0, keepdims=True)
        return m_new, l

    cols = heads * rows
    m0 = jnp.full((1, cols), -1e30, jnp.float32)
    l0 = jnp.zeros((1, cols), jnp.float32)
    m, l = lax.fori_loop(kb0, win, stat_step, (m0, l0))
    lse = m + jnp.log(l)

    def grad_step(c, carry):
        kc, st, allowed = scores(c)
        p = jnp.where(allowed, jnp.exp(st - lse), 0.0)
        vc = kvbuf[s, c, :, width:]
        dpt = lax.dot_general(vc, doall[...], nt, preferred_element_type=jnp.float32)
        ds = (p * (dpt - delta)).astype(jnp.bfloat16)
        pb = p.astype(jnp.bfloat16)
        dk = jnp.dot(ds, qall[...], preferred_element_type=jnp.float32) * scaling
        dv = jnp.dot(pb, doall[...], preferred_element_type=jnp.float32)
        dst = dst_ref[s * win + c]
        part_ref[dst, :, :width] += dk
        part_ref[dst, :, width:] += dv
        dqt[...] += lax.dot_general(kc, ds, tn, preferred_element_type=jnp.float32)
        return carry

    lax.fori_loop(kb0, win, grad_step, 0)
    for h in range(heads):
        piece = dqt[:, h * rows:(h + 1) * rows]
        dq_ref[:, h * width:(h + 1) * width] = (piece.T * scaling).astype(jnp.bfloat16)


def _shift(x, k, n, axis):
    return lax.ppermute(x, axis, [(i, (i + k) % n) for i in range(n)])


def _group_gather(x, n, axis):
    return jnp.stack([x] + [_shift(x, k, n, axis) for k in range(1, n)])


def _group_reduce(parts, n, axis, dim):
    me = lax.axis_index(axis)
    total = lax.dynamic_index_in_dim(parts, me, dim, keepdims=False).astype(jnp.float32)
    for k in range(1, n):
        piece = lax.dynamic_index_in_dim(parts, (me + k) % n, dim, keepdims=False)
        total = total + _shift(piece.astype(jnp.bfloat16), k, n, axis).astype(jnp.float32)
    return total


def body(queries, shared_keys, shared_values, outputs, out_grad, doc_lengths):
    n_in = lax.axis_size("w")
    rank = lax.axis_index("zp") * n_in + lax.axis_index("w")
    n_out = lax.axis_size("zp")
    n_seq = n_out * n_in
    rows = shared_keys.shape[0] // 2
    width = shared_keys.shape[1]
    heads = queries.shape[1] // width
    scaling = width ** (-0.5)
    win = REACH + 1
    doc_ends = jnp.cumsum(doc_lengths)
    doc_starts = doc_ends - doc_lengths
    blocks = jnp.stack([rank, 2 * n_seq - 1 - rank]).astype(jnp.int32)

    kv_local = jnp.concatenate([shared_keys, shared_values], axis=1)
    kv_col = _group_gather(kv_local, n_out, "zp")
    kv_recv = _group_gather(kv_col, n_in, "w").reshape(n_in * n_out * 2 * rows, 2 * width)

    me_z = lax.axis_index("zp")
    me_w = lax.axis_index("w")
    seq_blk = (blocks[:, None] - REACH + jnp.arange(win, dtype=jnp.int32)[None, :]).reshape(-1)
    seq_blk = jnp.maximum(seq_blk, 0)
    dev = jnp.where(seq_blk < n_seq, seq_blk, 2 * n_seq - 1 - seq_blk)
    slot = (seq_blk >= n_seq).astype(jnp.int32)
    k_z = (me_z - dev // n_in) % n_out
    k_w = (me_w - dev % n_in) % n_in
    srow = (((k_w * n_out + k_z) * 2 + slot) * rows).astype(jnp.int32)
    dst = (dev * 2 + slot).astype(jnp.int32)

    base_pos = jnp.arange(rows, dtype=jnp.int32)
    pos = blocks[:, None] * rows + base_pos[None, :]
    begins = jnp.max(
        jnp.where(doc_starts[None, None, :] <= pos[:, :, None], doc_starts[None, None, :], 0), axis=2
    ).astype(jnp.int32)
    kb0 = jnp.maximum(0, begins[:, 0] // rows - (blocks - REACH)).astype(jnp.int32)
    begin_t = jnp.tile(begins, (1, heads)).reshape(2, 1, heads * rows)
    qpos_t = jnp.tile(pos, (1, heads)).reshape(2, 1, heads * rows)
    prod = out_grad.astype(jnp.float32) * outputs.astype(jnp.float32)
    deltas = jnp.sum(prod.reshape(2, rows, heads, width), axis=3)
    delta_t = jnp.swapaxes(deltas, 1, 2).reshape(2, 1, heads * rows)

    kernel = functools.partial(
        _bwd_kernel, rows=rows, heads=heads, width=width, reach=REACH, scaling=scaling
    )
    cols = heads * rows
    vec = pl.BlockSpec((None, 1, cols), lambda s, *_: (s, 0, 0))
    grid_spec = pltpu.PrefetchScalarGridSpec(
        num_scalar_prefetch=4,
        grid=(2,),
        in_specs=[
            pl.BlockSpec((rows, cols), lambda s, *_: (s, 0)),
            pl.BlockSpec((rows, cols), lambda s, *_: (s, 0)),
            pl.BlockSpec(memory_space=pl.ANY),
            vec,
            vec,
            vec,
        ],
        out_specs=[
            pl.BlockSpec((rows, cols), lambda s, *_: (s, 0)),
            pl.BlockSpec((2 * n_seq, rows, 2 * width), lambda s, *_: (0, 0, 0)),
        ],
        scratch_shapes=[
            pltpu.VMEM((cols, width), jnp.bfloat16),
            pltpu.VMEM((cols, width), jnp.bfloat16),
            pltpu.VMEM((width, cols), jnp.float32),
            pltpu.VMEM((2, win, rows, 2 * width), jnp.bfloat16),
            pltpu.SemaphoreType.DMA((2, win)),
        ],
    )
    flops = 2 * 2 * win * 6 * rows * cols * width
    grad_queries, partial = pl.pallas_call(
        kernel,
        grid_spec=grid_spec,
        out_shape=[
            jax.ShapeDtypeStruct((2 * rows, cols), jnp.bfloat16),
            jax.ShapeDtypeStruct((2 * n_seq, rows, 2 * width), jnp.float32),
        ],
        compiler_params=pltpu.CompilerParams(dimension_semantics=("arbitrary",)),
        cost_estimate=pl.CostEstimate(
            flops=flops, transcendentals=2 * 2 * win * rows * cols, bytes_accessed=8 << 20
        ),
    )(blocks, kb0, srow, dst, queries, out_grad, kv_recv, begin_t, qpos_t, delta_t)

    storage = partial
    storage = storage.reshape(n_out, n_in, 2, rows, 2 * width).astype(jnp.bfloat16)
    plane = _group_reduce(storage, n_in, "w", 1)
    summed = _group_reduce(plane, n_out, "zp", 0).reshape(2 * rows, 2 * width)
    grad_keys = summed[:, :width].astype(jnp.bfloat16)
    grad_values = summed[:, width:].astype(jnp.bfloat16)
    return (grad_queries, grad_keys, grad_values)


GROUP = 4


def solution(mesh):
    n_seq, n_grp = mesh.devices.shape
    split = mesh.devices.reshape(n_seq // GROUP, GROUP, n_grp)
    mesh2 = jax.sharding.Mesh(split, ("zp", "w", "grp"))
    rows = P(("zp", "w"), "grp")
    placed = (rows, rows, rows, rows, rows, P())
    return jax.shard_map(
        body,
        mesh=mesh2,
        in_specs=placed,
        out_specs=(rows, rows, rows),
        check_vma=False,
    )
```

```python
import functools

import jax
import jax.numpy as jnp
from jax import lax
from jax.experimental import pallas as pl
from jax.experimental.pallas import tpu as pltpu
from jax.sharding import PartitionSpec as P

REACH = 16


def _bwd_kernel(blk_ref, starts_ref, srow_ref, dst_ref, q_ref, do_ref, kv_hbm,
                delta_ref, dq_ref, part_ref, qall, doall, dqt, kvbuf, sems,
                *, rows, heads, width, reach, scaling, docs):
    s = pl.program_id(0)
    win = reach + 1

    def copy(side, i):
        row = pl.multiple_of(srow_ref[side * win + i], rows)
        return pltpu.make_async_copy(
            kv_hbm.at[pl.ds(row, rows)], kvbuf.at[side, i], sems.at[side, i]
        )

    @pl.when(s == 0)
    def _():
        for side in range(2):
            for i in range(win):
                copy(side, i).start()
        part_ref[...] = jnp.zeros(part_ref.shape, jnp.float32)

    b = blk_ref[s]
    cols = heads * rows
    qpos = b * rows + lax.broadcasted_iota(jnp.int32, (1, cols), 1) % rows
    first = b * rows

    def doc_step(j, carry):
        vec, low = carry
        st = starts_ref[j]
        vec = jnp.where(st <= qpos, jnp.maximum(vec, st), vec)
        low = jnp.where(st <= first, jnp.maximum(low, st), low)
        return vec, low

    begin, low = lax.fori_loop(
        0, docs, doc_step, (jnp.zeros((1, cols), jnp.int32), jnp.int32(0))
    )
    kb0 = jnp.maximum(0, low // rows - (b - reach))
    for h in range(heads):
        qall[h * rows:(h + 1) * rows, :] = q_ref[:, h * width:(h + 1) * width]
        doall[h * rows:(h + 1) * rows, :] = do_ref[:, h * width:(h + 1) * width]
    delta = delta_ref[...]
    dqt[...] = jnp.zeros(dqt.shape, jnp.float32)
    k_iota = lax.broadcasted_iota(jnp.int32, (rows, 1), 0)
    base = (b - reach) * rows
    nt = (((1,), (1,)), ((), ()))
    tn = (((0,), (0,)), ((), ()))
    for i in range(win):
        copy(s, i).wait()

    def scores(c):
        kc = kvbuf[s, c, :, :width]
        st = lax.dot_general(kc, qall[...], nt, preferred_element_type=jnp.float32) * scaling
        kpos = base + c * rows + k_iota
        allowed = (kpos >= begin) & (kpos <= qpos)
        return kc, st, allowed

    def stat_step(c, carry):
        m, l = carry
        _, st, allowed = scores(c)
        masked = jnp.where(allowed, st, -1e30)
        m_new = jnp.maximum(m, jnp.max(masked, axis=0, keepdims=True))
        e = jnp.where(allowed, jnp.exp(st - m_new), 0.0)
        l = l * jnp.exp(m - m_new) + jnp.sum(e, axis=0, keepdims=True)
        return m_new, l

    m0 = jnp.full((1, cols), -1e30, jnp.float32)
    l0 = jnp.zeros((1, cols), jnp.float32)
    m, l = lax.fori_loop(kb0, win, stat_step, (m0, l0))
    lse = m + jnp.log(l)

    def grad_step(c, carry):
        kc, st, allowed = scores(c)
        p = jnp.where(allowed, jnp.exp(st - lse), 0.0)
        vc = kvbuf[s, c, :, width:]
        dpt = lax.dot_general(vc, doall[...], nt, preferred_element_type=jnp.float32)
        ds = (p * (dpt - delta)).astype(jnp.bfloat16)
        pb = p.astype(jnp.bfloat16)
        dk = jnp.dot(ds, qall[...], preferred_element_type=jnp.float32) * scaling
        dv = jnp.dot(pb, doall[...], preferred_element_type=jnp.float32)
        dst = dst_ref[s * win + c]
        part_ref[dst, :, :width] += dk
        part_ref[dst, :, width:] += dv
        dqt[...] += lax.dot_general(kc, ds, tn, preferred_element_type=jnp.float32)
        return carry

    lax.fori_loop(kb0, win, grad_step, 0)
    for h in range(heads):
        piece = dqt[:, h * rows:(h + 1) * rows]
        dq_ref[:, h * width:(h + 1) * width] = (piece.T * scaling).astype(jnp.bfloat16)


def _shift(x, k, n, axis):
    return lax.ppermute(x, axis, [(i, (i + k) % n) for i in range(n)])


def _group_gather(x, n, axis):
    return jnp.stack([x] + [_shift(x, k, n, axis) for k in range(1, n)])


def _group_reduce(parts, n, axis, dim):
    me = lax.axis_index(axis)
    total = lax.dynamic_index_in_dim(parts, me, dim, keepdims=False).astype(jnp.float32)
    for k in range(1, n):
        piece = lax.dynamic_index_in_dim(parts, (me + k) % n, dim, keepdims=False)
        total = total + _shift(piece.astype(jnp.bfloat16), k, n, axis).astype(jnp.float32)
    return total


def body(queries, shared_keys, shared_values, outputs, out_grad, doc_lengths):
    n_in = lax.axis_size("w")
    rank = lax.axis_index("zp") * n_in + lax.axis_index("w")
    n_out = lax.axis_size("zp")
    n_seq = n_out * n_in
    rows = shared_keys.shape[0] // 2
    width = shared_keys.shape[1]
    heads = queries.shape[1] // width
    scaling = width ** (-0.5)
    win = REACH + 1
    doc_ends = jnp.cumsum(doc_lengths)
    doc_starts = doc_ends - doc_lengths
    blocks = jnp.stack([rank, 2 * n_seq - 1 - rank]).astype(jnp.int32)

    kv_local = jnp.concatenate([shared_keys, shared_values], axis=1)
    kv_col = _group_gather(kv_local, n_out, "zp")
    kv_recv = _group_gather(kv_col, n_in, "w").reshape(n_in * n_out * 2 * rows, 2 * width)

    me_z = lax.axis_index("zp")
    me_w = lax.axis_index("w")
    seq_blk = (blocks[:, None] - REACH + jnp.arange(win, dtype=jnp.int32)[None, :]).reshape(-1)
    seq_blk = jnp.maximum(seq_blk, 0)
    dev = jnp.where(seq_blk < n_seq, seq_blk, 2 * n_seq - 1 - seq_blk)
    slot = (seq_blk >= n_seq).astype(jnp.int32)
    k_z = (me_z - dev // n_in) % n_out
    k_w = (me_w - dev % n_in) % n_in
    srow = (((k_w * n_out + k_z) * 2 + slot) * rows).astype(jnp.int32)
    dst = (dev * 2 + slot).astype(jnp.int32)

    prod = out_grad.astype(jnp.float32) * outputs.astype(jnp.float32)
    deltas = jnp.sum(prod.reshape(2, rows, heads, width), axis=3)
    delta_t = jnp.swapaxes(deltas, 1, 2).reshape(2, 1, heads * rows)

    kernel = functools.partial(
        _bwd_kernel, rows=rows, heads=heads, width=width, reach=REACH, scaling=scaling,
        docs=doc_lengths.shape[0],
    )
    cols = heads * rows
    vec = pl.BlockSpec((None, 1, cols), lambda s, *_: (s, 0, 0))
    grid_spec = pltpu.PrefetchScalarGridSpec(
        num_scalar_prefetch=4,
        grid=(2,),
        in_specs=[
            pl.BlockSpec((rows, cols), lambda s, *_: (s, 0)),
            pl.BlockSpec((rows, cols), lambda s, *_: (s, 0)),
            pl.BlockSpec(memory_space=pl.ANY),
            vec,
        ],
        out_specs=[
            pl.BlockSpec((rows, cols), lambda s, *_: (s, 0)),
            pl.BlockSpec((2 * n_seq, rows, 2 * width), lambda s, *_: (0, 0, 0)),
        ],
        scratch_shapes=[
            pltpu.VMEM((cols, width), jnp.bfloat16),
            pltpu.VMEM((cols, width), jnp.bfloat16),
            pltpu.VMEM((width, cols), jnp.float32),
            pltpu.VMEM((2, win, rows, 2 * width), jnp.bfloat16),
            pltpu.SemaphoreType.DMA((2, win)),
        ],
    )
    flops = 2 * 2 * win * 6 * rows * cols * width
    grad_queries, partial = pl.pallas_call(
        kernel,
        grid_spec=grid_spec,
        out_shape=[
            jax.ShapeDtypeStruct((2 * rows, cols), jnp.bfloat16),
            jax.ShapeDtypeStruct((2 * n_seq, rows, 2 * width), jnp.float32),
        ],
        compiler_params=pltpu.CompilerParams(dimension_semantics=("arbitrary",)),
        cost_estimate=pl.CostEstimate(
            flops=flops, transcendentals=2 * 2 * win * rows * cols, bytes_accessed=8 << 20
        ),
    )(blocks, doc_starts.astype(jnp.int32), srow, dst, queries, out_grad, kv_recv, delta_t)

    storage = partial
    storage = storage.reshape(n_out, n_in, 2, rows, 2 * width)
    plane = _group_reduce(storage, n_in, "w", 1)
    summed = _group_reduce(plane, n_out, "zp", 0).reshape(2 * rows, 2 * width)
    grad_keys = summed[:, :width].astype(jnp.bfloat16)
    grad_values = summed[:, width:].astype(jnp.bfloat16)
    return (grad_queries, grad_keys, grad_values)


GROUP = 4


def solution(mesh):
    n_seq, n_grp = mesh.devices.shape
    split = mesh.devices.reshape(n_seq // GROUP, GROUP, n_grp)
    mesh2 = jax.sharding.Mesh(split, ("zp", "w", "grp"))
    rows = P(("zp", "w"), "grp")
    placed = (rows, rows, rows, rows, rows, P())
    return jax.shard_map(
        body,
        mesh=mesh2,
        in_specs=placed,
        out_specs=(rows, rows, rows),
        check_vma=False,
    )
```

```python
import functools

import jax
import jax.numpy as jnp
from jax import lax
from jax.experimental import pallas as pl
from jax.experimental.pallas import tpu as pltpu
from jax.sharding import PartitionSpec as P

REACH = 16


def _bwd_kernel(blk_ref, starts_ref, srow_ref, dst_ref, q_ref, do_ref, kv_hbm,
                delta_ref, dq_ref, part_ref, qall, doall, dqt, kvbuf, sems, sbuf,
                *, rows, heads, width, reach, scaling, docs):
    s = pl.program_id(0)
    win = reach + 1

    def copy(side, i):
        row = pl.multiple_of(srow_ref[side * win + i], rows)
        return pltpu.make_async_copy(
            kv_hbm.at[pl.ds(row, rows)], kvbuf.at[side, i], sems.at[side, i]
        )

    @pl.when(s == 0)
    def _():
        for side in range(2):
            for i in range(win):
                copy(side, i).start()
        part_ref[...] = jnp.zeros(part_ref.shape, jnp.float32)

    b = blk_ref[s]
    cols = heads * rows
    qpos = b * rows + lax.broadcasted_iota(jnp.int32, (1, cols), 1) % rows
    first = b * rows

    def doc_step(j, carry):
        vec, low = carry
        st = starts_ref[j]
        vec = jnp.where(st <= qpos, jnp.maximum(vec, st), vec)
        low = jnp.where(st <= first, jnp.maximum(low, st), low)
        return vec, low

    begin, low = lax.fori_loop(
        0, docs, doc_step, (jnp.zeros((1, cols), jnp.int32), jnp.int32(0))
    )
    kb0 = jnp.maximum(0, low // rows - (b - reach))
    for h in range(heads):
        qall[h * rows:(h + 1) * rows, :] = q_ref[:, h * width:(h + 1) * width]
        doall[h * rows:(h + 1) * rows, :] = do_ref[:, h * width:(h + 1) * width]
    delta = delta_ref[...]
    dqt[...] = jnp.zeros(dqt.shape, jnp.float32)
    k_iota = lax.broadcasted_iota(jnp.int32, (rows, 1), 0)
    base = (b - reach) * rows
    nt = (((1,), (1,)), ((), ()))
    tn = (((0,), (0,)), ((), ()))
    for i in range(win):
        copy(s, i).wait()

    def scores(c):
        kc = kvbuf[s, c, :, :width]
        st = lax.dot_general(kc, qall[...], nt, preferred_element_type=jnp.float32) * scaling
        kpos = base + c * rows + k_iota
        allowed = (kpos >= begin) & (kpos <= qpos)
        return kc, st, allowed

    def stat_step(c, m):
        _, st, allowed = scores(c)
        masked = jnp.where(allowed, st, -1e30)
        sbuf[c] = masked
        return jnp.maximum(m, jnp.max(masked, axis=0, keepdims=True))

    m0 = jnp.full((1, cols), -1e30, jnp.float32)
    l0 = jnp.zeros((1, cols), jnp.float32)
    m = lax.fori_loop(kb0, win, stat_step, m0)

    def exp_step(c, l):
        e = jnp.exp(sbuf[c] - m)
        sbuf[c] = e
        return l + jnp.sum(e, axis=0, keepdims=True)

    inv_l = 1.0 / lax.fori_loop(kb0, win, exp_step, l0)

    def grad_step(c, carry):
        kc = kvbuf[s, c, :, :width]
        p = sbuf[c] * inv_l
        vc = kvbuf[s, c, :, width:]
        dpt = lax.dot_general(vc, doall[...], nt, preferred_element_type=jnp.float32)
        ds = (p * (dpt - delta)).astype(jnp.bfloat16)
        pb = p.astype(jnp.bfloat16)
        dk = jnp.dot(ds, qall[...], preferred_element_type=jnp.float32) * scaling
        dv = jnp.dot(pb, doall[...], preferred_element_type=jnp.float32)
        dst = dst_ref[s * win + c]
        part_ref[dst, :, :width] += dk
        part_ref[dst, :, width:] += dv
        dqt[...] += lax.dot_general(kc, ds, tn, preferred_element_type=jnp.float32)
        return carry

    lax.fori_loop(kb0, win, grad_step, 0)
    for h in range(heads):
        piece = dqt[:, h * rows:(h + 1) * rows]
        dq_ref[:, h * width:(h + 1) * width] = (piece.T * scaling).astype(jnp.bfloat16)


def _shift(x, k, n, axis):
    return lax.ppermute(x, axis, [(i, (i + k) % n) for i in range(n)])


def _group_gather(x, n, axis):
    return jnp.stack([x] + [_shift(x, k, n, axis) for k in range(1, n)])


def _group_reduce(parts, n, axis, dim):
    me = lax.axis_index(axis)
    total = lax.dynamic_index_in_dim(parts, me, dim, keepdims=False).astype(jnp.float32)
    for k in range(1, n):
        piece = lax.dynamic_index_in_dim(parts, (me + k) % n, dim, keepdims=False)
        total = total + _shift(piece.astype(jnp.bfloat16), k, n, axis).astype(jnp.float32)
    return total


def body(queries, shared_keys, shared_values, outputs, out_grad, doc_lengths):
    n_in = lax.axis_size("w")
    rank = lax.axis_index("zp") * n_in + lax.axis_index("w")
    n_out = lax.axis_size("zp")
    n_seq = n_out * n_in
    rows = shared_keys.shape[0] // 2
    width = shared_keys.shape[1]
    heads = queries.shape[1] // width
    scaling = width ** (-0.5)
    win = REACH + 1
    doc_ends = jnp.cumsum(doc_lengths)
    doc_starts = doc_ends - doc_lengths
    blocks = jnp.stack([rank, 2 * n_seq - 1 - rank]).astype(jnp.int32)

    kv_local = jnp.concatenate([shared_keys, shared_values], axis=1)
    kv_col = _group_gather(kv_local, n_out, "zp")
    kv_recv = _group_gather(kv_col, n_in, "w").reshape(n_in * n_out * 2 * rows, 2 * width)

    me_z = lax.axis_index("zp")
    me_w = lax.axis_index("w")
    seq_blk = (blocks[:, None] - REACH + jnp.arange(win, dtype=jnp.int32)[None, :]).reshape(-1)
    seq_blk = jnp.maximum(seq_blk, 0)
    dev = jnp.where(seq_blk < n_seq, seq_blk, 2 * n_seq - 1 - seq_blk)
    slot = (seq_blk >= n_seq).astype(jnp.int32)
    k_z = (me_z - dev // n_in) % n_out
    k_w = (me_w - dev % n_in) % n_in
    srow = (((k_w * n_out + k_z) * 2 + slot) * rows).astype(jnp.int32)
    dst = (dev * 2 + slot).astype(jnp.int32)

    prod = out_grad.astype(jnp.float32) * outputs.astype(jnp.float32)
    deltas = jnp.sum(prod.reshape(2, rows, heads, width), axis=3)
    delta_t = jnp.swapaxes(deltas, 1, 2).reshape(2, 1, heads * rows)

    kernel = functools.partial(
        _bwd_kernel, rows=rows, heads=heads, width=width, reach=REACH, scaling=scaling,
        docs=doc_lengths.shape[0],
    )
    cols = heads * rows
    vec = pl.BlockSpec((None, 1, cols), lambda s, *_: (s, 0, 0))
    grid_spec = pltpu.PrefetchScalarGridSpec(
        num_scalar_prefetch=4,
        grid=(2,),
        in_specs=[
            pl.BlockSpec((rows, cols), lambda s, *_: (s, 0)),
            pl.BlockSpec((rows, cols), lambda s, *_: (s, 0)),
            pl.BlockSpec(memory_space=pl.ANY),
            vec,
        ],
        out_specs=[
            pl.BlockSpec((rows, cols), lambda s, *_: (s, 0)),
            pl.BlockSpec((2 * n_seq, rows, 2 * width), lambda s, *_: (0, 0, 0)),
        ],
        scratch_shapes=[
            pltpu.VMEM((cols, width), jnp.bfloat16),
            pltpu.VMEM((cols, width), jnp.bfloat16),
            pltpu.VMEM((width, cols), jnp.float32),
            pltpu.VMEM((2, win, rows, 2 * width), jnp.bfloat16),
            pltpu.SemaphoreType.DMA((2, win)),
            pltpu.VMEM((win, rows, cols), jnp.float32),
        ],
    )
    flops = 2 * 2 * win * 6 * rows * cols * width
    grad_queries, partial = pl.pallas_call(
        kernel,
        grid_spec=grid_spec,
        out_shape=[
            jax.ShapeDtypeStruct((2 * rows, cols), jnp.bfloat16),
            jax.ShapeDtypeStruct((2 * n_seq, rows, 2 * width), jnp.float32),
        ],
        compiler_params=pltpu.CompilerParams(dimension_semantics=("arbitrary",)),
        cost_estimate=pl.CostEstimate(
            flops=flops, transcendentals=2 * 2 * win * rows * cols, bytes_accessed=8 << 20
        ),
    )(blocks, doc_starts.astype(jnp.int32), srow, dst, queries, out_grad, kv_recv, delta_t)

    storage = partial
    storage = storage.reshape(n_out, n_in, 2, rows, 2 * width)
    plane = _group_reduce(storage, n_in, "w", 1)
    summed = _group_reduce(plane, n_out, "zp", 0).reshape(2 * rows, 2 * width)
    grad_keys = summed[:, :width].astype(jnp.bfloat16)
    grad_values = summed[:, width:].astype(jnp.bfloat16)
    return (grad_queries, grad_keys, grad_values)


GROUP = 4


def solution(mesh):
    n_seq, n_grp = mesh.devices.shape
    split = mesh.devices.reshape(n_seq // GROUP, GROUP, n_grp)
    mesh2 = jax.sharding.Mesh(split, ("zp", "w", "grp"))
    rows = P(("zp", "w"), "grp")
    placed = (rows, rows, rows, rows, rows, P())
    return jax.shard_map(
        body,
        mesh=mesh2,
        in_specs=placed,
        out_specs=(rows, rows, rows),
        check_vma=False,
    )
```

```python
import functools

import jax
import jax.numpy as jnp
from jax import lax
from jax.experimental import pallas as pl
from jax.experimental.pallas import tpu as pltpu
from jax.sharding import PartitionSpec as P

REACH = 16


def _bwd_kernel(blk_ref, starts_ref, srow_ref, dst_ref, q_ref, do_ref, kv_hbm,
                delta_ref, dq_ref, part_ref, qall, doall, dqt, kvbuf, sems, sbuf, dsbuf,
                *, rows, heads, width, reach, scaling, docs):
    s = pl.program_id(0)
    win = reach + 1

    def copy(side, i):
        row = pl.multiple_of(srow_ref[side * win + i], rows)
        return pltpu.make_async_copy(
            kv_hbm.at[pl.ds(row, rows)], kvbuf.at[side, i], sems.at[side, i]
        )

    @pl.when(s == 0)
    def _():
        for side in range(2):
            for i in range(win):
                copy(side, i).start()
        part_ref[...] = jnp.zeros(part_ref.shape, jnp.float32)

    b = blk_ref[s]
    cols = heads * rows
    qpos = b * rows + lax.broadcasted_iota(jnp.int32, (1, cols), 1) % rows
    first = b * rows

    def doc_step(j, carry):
        vec, low = carry
        st = starts_ref[j]
        vec = jnp.where(st <= qpos, jnp.maximum(vec, st), vec)
        low = jnp.where(st <= first, jnp.maximum(low, st), low)
        return vec, low

    begin, low = lax.fori_loop(
        0, docs, doc_step, (jnp.zeros((1, cols), jnp.int32), jnp.int32(0))
    )
    kb0 = jnp.maximum(0, low // rows - (b - reach))
    for h in range(heads):
        qall[h * rows:(h + 1) * rows, :] = q_ref[:, h * width:(h + 1) * width]
        doall[h * rows:(h + 1) * rows, :] = do_ref[:, h * width:(h + 1) * width]
    delta = delta_ref[...]
    k_iota = lax.broadcasted_iota(jnp.int32, (rows, 1), 0)
    base = (b - reach) * rows
    nt = (((1,), (1,)), ((), ()))
    tn = (((0,), (0,)), ((), ()))
    for i in range(win):
        copy(s, i).wait()

    def scores(c):
        kc = kvbuf[s, c, :, :width]
        st = lax.dot_general(kc, qall[...], nt, preferred_element_type=jnp.float32) * scaling
        kpos = base + c * rows + k_iota
        allowed = (kpos >= begin) & (kpos <= qpos)
        return kc, st, allowed

    def stat_step(c, m):
        _, st, allowed = scores(c)
        masked = jnp.where(allowed, st, -1e30)
        sbuf[c] = masked
        return jnp.maximum(m, jnp.max(masked, axis=0, keepdims=True))

    m0 = jnp.full((1, cols), -1e30, jnp.float32)
    l0 = jnp.zeros((1, cols), jnp.float32)
    m = lax.fori_loop(kb0, win, stat_step, m0)

    def exp_step(c, l):
        e = jnp.exp(sbuf[c] - m)
        sbuf[c] = e
        return l + jnp.sum(e, axis=0, keepdims=True)

    inv_l = 1.0 / lax.fori_loop(kb0, win, exp_step, l0)

    def grad_step(c, carry):
        p = sbuf[c] * inv_l
        vc = kvbuf[s, c, :, width:]
        dpt = lax.dot_general(vc, doall[...], nt, preferred_element_type=jnp.float32)
        ds = (p * (dpt - delta)).astype(jnp.bfloat16)
        pb = p.astype(jnp.bfloat16)
        dk = jnp.dot(ds, qall[...], preferred_element_type=jnp.float32) * scaling
        dv = jnp.dot(pb, doall[...], preferred_element_type=jnp.float32)
        dst = dst_ref[s * win + c]
        part_ref[dst, :, :width] += dk
        part_ref[dst, :, width:] += dv
        dsbuf[c] = ds
        return carry

    lax.fori_loop(kb0, win, grad_step, 0)

    def clear_step(c, carry):
        dsbuf[c] = jnp.zeros((rows, cols), jnp.bfloat16)
        return carry

    lax.fori_loop(0, kb0, clear_step, 0)
    kwin = kvbuf[s, :, :, :width].reshape(win * rows, width)
    dqt[...] = lax.dot_general(
        kwin, dsbuf[...].reshape(win * rows, cols), tn, preferred_element_type=jnp.float32
    )
    for h in range(heads):
        piece = dqt[:, h * rows:(h + 1) * rows]
        dq_ref[:, h * width:(h + 1) * width] = (piece.T * scaling).astype(jnp.bfloat16)


def _shift(x, k, n, axis):
    return lax.ppermute(x, axis, [(i, (i + k) % n) for i in range(n)])


def _group_gather(x, n, axis):
    return jnp.stack([x] + [_shift(x, k, n, axis) for k in range(1, n)])


def _group_reduce(parts, n, axis, dim):
    me = lax.axis_index(axis)
    total = lax.dynamic_index_in_dim(parts, me, dim, keepdims=False).astype(jnp.float32)
    for k in range(1, n):
        piece = lax.dynamic_index_in_dim(parts, (me + k) % n, dim, keepdims=False)
        total = total + _shift(piece.astype(jnp.bfloat16), k, n, axis).astype(jnp.float32)
    return total


def body(queries, shared_keys, shared_values, outputs, out_grad, doc_lengths):
    n_in = lax.axis_size("w")
    rank = lax.axis_index("zp") * n_in + lax.axis_index("w")
    n_out = lax.axis_size("zp")
    n_seq = n_out * n_in
    rows = shared_keys.shape[0] // 2
    width = shared_keys.shape[1]
    heads = queries.shape[1] // width
    scaling = width ** (-0.5)
    win = REACH + 1
    doc_ends = jnp.cumsum(doc_lengths)
    doc_starts = doc_ends - doc_lengths
    blocks = jnp.stack([rank, 2 * n_seq - 1 - rank]).astype(jnp.int32)

    kv_local = jnp.concatenate([shared_keys, shared_values], axis=1)
    kv_col = _group_gather(kv_local, n_out, "zp")
    kv_recv = _group_gather(kv_col, n_in, "w").reshape(n_in * n_out * 2 * rows, 2 * width)

    me_z = lax.axis_index("zp")
    me_w = lax.axis_index("w")
    seq_blk = (blocks[:, None] - REACH + jnp.arange(win, dtype=jnp.int32)[None, :]).reshape(-1)
    seq_blk = jnp.maximum(seq_blk, 0)
    dev = jnp.where(seq_blk < n_seq, seq_blk, 2 * n_seq - 1 - seq_blk)
    slot = (seq_blk >= n_seq).astype(jnp.int32)
    k_z = (me_z - dev // n_in) % n_out
    k_w = (me_w - dev % n_in) % n_in
    srow = (((k_w * n_out + k_z) * 2 + slot) * rows).astype(jnp.int32)
    dst = (dev * 2 + slot).astype(jnp.int32)

    prod = out_grad.astype(jnp.float32) * outputs.astype(jnp.float32)
    deltas = jnp.sum(prod.reshape(2, rows, heads, width), axis=3)
    delta_t = jnp.swapaxes(deltas, 1, 2).reshape(2, 1, heads * rows)

    kernel = functools.partial(
        _bwd_kernel, rows=rows, heads=heads, width=width, reach=REACH, scaling=scaling,
        docs=doc_lengths.shape[0],
    )
    cols = heads * rows
    vec = pl.BlockSpec((None, 1, cols), lambda s, *_: (s, 0, 0))
    grid_spec = pltpu.PrefetchScalarGridSpec(
        num_scalar_prefetch=4,
        grid=(2,),
        in_specs=[
            pl.BlockSpec((rows, cols), lambda s, *_: (s, 0)),
            pl.BlockSpec((rows, cols), lambda s, *_: (s, 0)),
            pl.BlockSpec(memory_space=pl.ANY),
            vec,
        ],
        out_specs=[
            pl.BlockSpec((rows, cols), lambda s, *_: (s, 0)),
            pl.BlockSpec((2 * n_seq, rows, 2 * width), lambda s, *_: (0, 0, 0)),
        ],
        scratch_shapes=[
            pltpu.VMEM((cols, width), jnp.bfloat16),
            pltpu.VMEM((cols, width), jnp.bfloat16),
            pltpu.VMEM((width, cols), jnp.float32),
            pltpu.VMEM((2, win, rows, 2 * width), jnp.bfloat16),
            pltpu.SemaphoreType.DMA((2, win)),
            pltpu.VMEM((win, rows, cols), jnp.float32),
            pltpu.VMEM((win, rows, cols), jnp.bfloat16),
        ],
    )
    flops = 2 * 2 * win * 6 * rows * cols * width
    grad_queries, partial = pl.pallas_call(
        kernel,
        grid_spec=grid_spec,
        out_shape=[
            jax.ShapeDtypeStruct((2 * rows, cols), jnp.bfloat16),
            jax.ShapeDtypeStruct((2 * n_seq, rows, 2 * width), jnp.float32),
        ],
        compiler_params=pltpu.CompilerParams(dimension_semantics=("arbitrary",)),
        cost_estimate=pl.CostEstimate(
            flops=flops, transcendentals=2 * 2 * win * rows * cols, bytes_accessed=8 << 20
        ),
    )(blocks, doc_starts.astype(jnp.int32), srow, dst, queries, out_grad, kv_recv, delta_t)

    storage = partial
    storage = storage.reshape(n_out, n_in, 2, rows, 2 * width)
    plane = _group_reduce(storage, n_in, "w", 1)
    summed = _group_reduce(plane, n_out, "zp", 0).reshape(2 * rows, 2 * width)
    grad_keys = summed[:, :width].astype(jnp.bfloat16)
    grad_values = summed[:, width:].astype(jnp.bfloat16)
    return (grad_queries, grad_keys, grad_values)


GROUP = 4


def solution(mesh):
    n_seq, n_grp = mesh.devices.shape
    split = mesh.devices.reshape(n_seq // GROUP, GROUP, n_grp)
    mesh2 = jax.sharding.Mesh(split, ("zp", "w", "grp"))
    rows = P(("zp", "w"), "grp")
    placed = (rows, rows, rows, rows, rows, P())
    return jax.shard_map(
        body,
        mesh=mesh2,
        in_specs=placed,
        out_specs=(rows, rows, rows),
        check_vma=False,
    )
```

```python
import functools

import jax
import jax.numpy as jnp
from jax import lax
from jax.experimental import pallas as pl
from jax.experimental.pallas import tpu as pltpu
from jax.sharding import PartitionSpec as P

REACH = 16


def _bwd_kernel(blk_ref, starts_ref, srow_ref, dst_ref, q_ref, do_ref, kv_hbm,
                delta_ref, dq_ref, part_ref, qall, doall, dqt, kvbuf, sems, sbuf, dsbuf,
                bounds, *, rows, heads, width, reach, scaling, docs, n_seq):
    s = pl.program_id(0)
    win = reach + 1
    cols = heads * rows

    def copy(side, i):
        row = pl.multiple_of(srow_ref[side * win + i], rows)
        return pltpu.make_async_copy(
            kv_hbm.at[pl.ds(row, rows)], kvbuf.at[side, i], sems.at[side, i]
        )

    def seq_of(d):
        dev = d // 2
        return jnp.where(d % 2 == 0, dev, 2 * n_seq - 1 - dev)

    def touched(side, j):
        top = blk_ref[side]
        return (j >= top - reach + bounds[2 * side]) & (j <= top)

    @pl.when(s == 0)
    def _():
        for side in range(2):
            for i in range(win):
                copy(side, i).start()

        def bound_step(j, carry):
            st = starts_ref[j]
            out = []
            for side in range(2):
                first = blk_ref[side] * rows
                lo, hi = carry[2 * side], carry[2 * side + 1]
                out.append(jnp.where(st <= first, jnp.maximum(lo, st), lo))
                out.append(jnp.where(st <= first + rows - 1, jnp.maximum(hi, st), hi))
            return tuple(out)

        found = lax.fori_loop(0, docs, bound_step, (jnp.int32(0),) * 4)
        for side in range(2):
            top = blk_ref[side]
            base_side = (top - reach) * rows
            kb0_side = jnp.maximum(0, found[2 * side] // rows - (top - reach))
            free = (found[2 * side + 1] - base_side + rows - 1) // rows
            bounds[2 * side] = kb0_side
            bounds[2 * side + 1] = jnp.minimum(reach, jnp.maximum(kb0_side, free))

        def zero_step(d, carry):
            j = seq_of(d)

            @pl.when(jnp.logical_not(touched(0, j) | touched(1, j)))
            def _():
                part_ref[d] = jnp.zeros((rows, 2 * width), jnp.float32)

            return carry

        lax.fori_loop(0, 2 * n_seq, zero_step, 0)

    b = blk_ref[s]
    kb0 = bounds[2 * s]
    c_free = bounds[2 * s + 1]
    qpos = b * rows + lax.broadcasted_iota(jnp.int32, (1, cols), 1) % rows

    def doc_step(j, vec):
        st = starts_ref[j]
        return jnp.where(st <= qpos, jnp.maximum(vec, st), vec)

    begin = lax.fori_loop(0, docs, doc_step, jnp.zeros((1, cols), jnp.int32))
    for h in range(heads):
        qall[h * rows:(h + 1) * rows, :] = q_ref[:, h * width:(h + 1) * width]
        doall[h * rows:(h + 1) * rows, :] = do_ref[:, h * width:(h + 1) * width]
    delta = delta_ref[...]
    k_iota = lax.broadcasted_iota(jnp.int32, (rows, 1), 0)
    base = (b - reach) * rows
    nt = (((1,), (1,)), ((), ()))
    tn = (((0,), (0,)), ((), ()))
    for i in range(win):
        copy(s, i).wait()

    def stat_masked(c, m):
        kc = kvbuf[s, c, :, :width]
        st = lax.dot_general(kc, qall[...], nt, preferred_element_type=jnp.float32) * scaling
        kpos = base + c * rows + k_iota
        allowed = (kpos >= begin) & (kpos <= qpos)
        masked = jnp.where(allowed, st, -1e30)
        sbuf[c] = masked
        return jnp.maximum(m, jnp.max(masked, axis=0, keepdims=True))

    def stat_free(c, m):
        kc = kvbuf[s, c, :, :width]
        st = lax.dot_general(kc, qall[...], nt, preferred_element_type=jnp.float32) * scaling
        sbuf[c] = st
        return jnp.maximum(m, jnp.max(st, axis=0, keepdims=True))

    m0 = jnp.full((1, cols), -1e30, jnp.float32)
    l0 = jnp.zeros((1, cols), jnp.float32)
    m = lax.fori_loop(kb0, c_free, stat_masked, m0)
    m = lax.fori_loop(c_free, reach, stat_free, m)
    m = stat_masked(reach, m)

    def exp_step(c, l):
        e = jnp.exp(sbuf[c] - m)
        sbuf[c] = e
        return l + jnp.sum(e, axis=0, keepdims=True)

    inv_l = 1.0 / lax.fori_loop(kb0, win, exp_step, l0)

    def grad_step(c, carry):
        p = sbuf[c] * inv_l
        vc = kvbuf[s, c, :, width:]
        dpt = lax.dot_general(vc, doall[...], nt, preferred_element_type=jnp.float32)
        ds = (p * (dpt - delta)).astype(jnp.bfloat16)
        pb = p.astype(jnp.bfloat16)
        dk = jnp.dot(ds, qall[...], preferred_element_type=jnp.float32) * scaling
        dv = jnp.dot(pb, doall[...], preferred_element_type=jnp.float32)
        dst = dst_ref[s * win + c]
        add = (s == 1) & touched(0, b - reach + c)

        @pl.when(add)
        def _():
            part_ref[dst, :, :width] += dk
            part_ref[dst, :, width:] += dv

        @pl.when(jnp.logical_not(add))
        def _():
            part_ref[dst, :, :width] = dk
            part_ref[dst, :, width:] = dv

        dsbuf[c] = ds
        return carry

    lax.fori_loop(kb0, win, grad_step, 0)

    def clear_step(c, carry):
        dsbuf[c] = jnp.zeros((rows, cols), jnp.bfloat16)
        return carry

    lax.fori_loop(0, kb0, clear_step, 0)
    kwin = kvbuf[s, :, :, :width].reshape(win * rows, width)
    dqt[...] = lax.dot_general(
        kwin, dsbuf[...].reshape(win * rows, cols), tn, preferred_element_type=jnp.float32
    )
    for h in range(heads):
        piece = dqt[:, h * rows:(h + 1) * rows]
        dq_ref[:, h * width:(h + 1) * width] = (piece.T * scaling).astype(jnp.bfloat16)


def _shift(x, k, n, axis):
    return lax.ppermute(x, axis, [(i, (i + k) % n) for i in range(n)])


def _group_gather(x, n, axis):
    return jnp.stack([x] + [_shift(x, k, n, axis) for k in range(1, n)])


def _group_reduce(parts, n, axis, dim):
    me = lax.axis_index(axis)
    total = lax.dynamic_index_in_dim(parts, me, dim, keepdims=False).astype(jnp.float32)
    for k in range(1, n):
        piece = lax.dynamic_index_in_dim(parts, (me + k) % n, dim, keepdims=False)
        total = total + _shift(piece.astype(jnp.bfloat16), k, n, axis).astype(jnp.float32)
    return total


def body(queries, shared_keys, shared_values, outputs, out_grad, doc_lengths):
    n_in = lax.axis_size("w")
    rank = lax.axis_index("zp") * n_in + lax.axis_index("w")
    n_out = lax.axis_size("zp")
    n_seq = n_out * n_in
    rows = shared_keys.shape[0] // 2
    width = shared_keys.shape[1]
    heads = queries.shape[1] // width
    scaling = width ** (-0.5)
    win = REACH + 1
    doc_ends = jnp.cumsum(doc_lengths)
    doc_starts = doc_ends - doc_lengths
    blocks = jnp.stack([rank, 2 * n_seq - 1 - rank]).astype(jnp.int32)

    kv_local = jnp.concatenate([shared_keys, shared_values], axis=1)
    kv_col = _group_gather(kv_local, n_out, "zp")
    kv_recv = _group_gather(kv_col, n_in, "w").reshape(n_in * n_out * 2 * rows, 2 * width)

    me_z = lax.axis_index("zp")
    me_w = lax.axis_index("w")
    seq_blk = (blocks[:, None] - REACH + jnp.arange(win, dtype=jnp.int32)[None, :]).reshape(-1)
    seq_blk = jnp.maximum(seq_blk, 0)
    dev = jnp.where(seq_blk < n_seq, seq_blk, 2 * n_seq - 1 - seq_blk)
    slot = (seq_blk >= n_seq).astype(jnp.int32)
    k_z = (me_z - dev // n_in) % n_out
    k_w = (me_w - dev % n_in) % n_in
    srow = (((k_w * n_out + k_z) * 2 + slot) * rows).astype(jnp.int32)
    dst = (dev * 2 + slot).astype(jnp.int32)

    prod = out_grad.astype(jnp.float32) * outputs.astype(jnp.float32)
    deltas = jnp.sum(prod.reshape(2, rows, heads, width), axis=3)
    delta_t = jnp.swapaxes(deltas, 1, 2).reshape(2, 1, heads * rows)

    kernel = functools.partial(
        _bwd_kernel, rows=rows, heads=heads, width=width, reach=REACH, scaling=scaling,
        docs=doc_lengths.shape[0], n_seq=n_seq,
    )
    cols = heads * rows
    vec = pl.BlockSpec((None, 1, cols), lambda s, *_: (s, 0, 0))
    grid_spec = pltpu.PrefetchScalarGridSpec(
        num_scalar_prefetch=4,
        grid=(2,),
        in_specs=[
            pl.BlockSpec((rows, cols), lambda s, *_: (s, 0)),
            pl.BlockSpec((rows, cols), lambda s, *_: (s, 0)),
            pl.BlockSpec(memory_space=pl.ANY),
            vec,
        ],
        out_specs=[
            pl.BlockSpec((rows, cols), lambda s, *_: (s, 0)),
            pl.BlockSpec((2 * n_seq, rows, 2 * width), lambda s, *_: (0, 0, 0)),
        ],
        scratch_shapes=[
            pltpu.VMEM((cols, width), jnp.bfloat16),
            pltpu.VMEM((cols, width), jnp.bfloat16),
            pltpu.VMEM((width, cols), jnp.float32),
            pltpu.VMEM((2, win, rows, 2 * width), jnp.bfloat16),
            pltpu.SemaphoreType.DMA((2, win)),
            pltpu.VMEM((win, rows, cols), jnp.float32),
            pltpu.VMEM((win, rows, cols), jnp.bfloat16),
            pltpu.SMEM((4,), jnp.int32),
        ],
    )
    flops = 2 * 2 * win * 6 * rows * cols * width
    grad_queries, partial = pl.pallas_call(
        kernel,
        grid_spec=grid_spec,
        out_shape=[
            jax.ShapeDtypeStruct((2 * rows, cols), jnp.bfloat16),
            jax.ShapeDtypeStruct((2 * n_seq, rows, 2 * width), jnp.float32),
        ],
        compiler_params=pltpu.CompilerParams(dimension_semantics=("arbitrary",)),
        cost_estimate=pl.CostEstimate(
            flops=flops, transcendentals=2 * 2 * win * rows * cols, bytes_accessed=8 << 20
        ),
    )(blocks, doc_starts.astype(jnp.int32), srow, dst, queries, out_grad, kv_recv, delta_t)

    storage = partial
    storage = storage.reshape(n_out, n_in, 2, rows, 2 * width)
    plane = _group_reduce(storage, n_in, "w", 1)
    summed = _group_reduce(plane, n_out, "zp", 0).reshape(2 * rows, 2 * width)
    grad_keys = summed[:, :width].astype(jnp.bfloat16)
    grad_values = summed[:, width:].astype(jnp.bfloat16)
    return (grad_queries, grad_keys, grad_values)


GROUP = 4


def solution(mesh):
    n_seq, n_grp = mesh.devices.shape
    split = mesh.devices.reshape(n_seq // GROUP, GROUP, n_grp)
    mesh2 = jax.sharding.Mesh(split, ("zp", "w", "grp"))
    rows = P(("zp", "w"), "grp")
    placed = (rows, rows, rows, rows, rows, P())
    return jax.shard_map(
        body,
        mesh=mesh2,
        in_specs=placed,
        out_specs=(rows, rows, rows),
        check_vma=False,
    )
```

```python
import functools

import jax
import jax.numpy as jnp
from jax import lax
from jax.experimental import pallas as pl
from jax.experimental.pallas import tpu as pltpu
from jax.sharding import PartitionSpec as P

REACH = 16


def _bwd_kernel(blk_ref, starts_ref, srow_ref, src_ref, dst_ref, q_ref, do_ref, *rest,
                rows, heads, width, reach, scaling, docs, pieces):
    kv_refs = rest[:pieces]
    (delta_ref, dq_ref, part_ref, qall, doall, dqt, kvbuf, sems, sbuf, dsbuf) = rest[pieces:]
    s = pl.program_id(0)
    win = reach + 1

    def copy(side, i, ref):
        row = pl.multiple_of(srow_ref[side * win + i], rows)
        return pltpu.make_async_copy(
            ref.at[pl.ds(row, rows)], kvbuf.at[side, i], sems.at[side, i]
        )

    @pl.when(s == 0)
    def _():
        for side in range(2):
            for i in range(win):
                which = src_ref[side * win + i]
                for t in range(pieces):
                    @pl.when(which == t)
                    def _():
                        copy(side, i, kv_refs[t]).start()
        part_ref[...] = jnp.zeros(part_ref.shape, jnp.float32)

    b = blk_ref[s]
    cols = heads * rows
    qpos = b * rows + lax.broadcasted_iota(jnp.int32, (1, cols), 1) % rows
    first = b * rows

    def doc_step(j, carry):
        vec, low = carry
        st = starts_ref[j]
        vec = jnp.where(st <= qpos, jnp.maximum(vec, st), vec)
        low = jnp.where(st <= first, jnp.maximum(low, st), low)
        return vec, low

    begin, low = lax.fori_loop(
        0, docs, doc_step, (jnp.zeros((1, cols), jnp.int32), jnp.int32(0))
    )
    kb0 = jnp.maximum(0, low // rows - (b - reach))
    for h in range(heads):
        qall[h * rows:(h + 1) * rows, :] = q_ref[:, h * width:(h + 1) * width]
        doall[h * rows:(h + 1) * rows, :] = do_ref[:, h * width:(h + 1) * width]
    delta = delta_ref[...]
    k_iota = lax.broadcasted_iota(jnp.int32, (rows, 1), 0)
    base = (b - reach) * rows
    nt = (((1,), (1,)), ((), ()))
    tn = (((0,), (0,)), ((), ()))
    for i in range(win):
        copy(s, i, kv_refs[0]).wait()

    def scores(c):
        kc = kvbuf[s, c, :, :width]
        st = lax.dot_general(kc, qall[...], nt, preferred_element_type=jnp.float32) * scaling
        kpos = base + c * rows + k_iota
        allowed = (kpos >= begin) & (kpos <= qpos)
        return kc, st, allowed

    def stat_step(c, m):
        _, st, allowed = scores(c)
        masked = jnp.where(allowed, st, -1e30)
        sbuf[c] = masked
        return jnp.maximum(m, jnp.max(masked, axis=0, keepdims=True))

    m0 = jnp.full((1, cols), -1e30, jnp.float32)
    l0 = jnp.zeros((1, cols), jnp.float32)
    m = lax.fori_loop(kb0, win, stat_step, m0)

    def exp_step(c, l):
        e = jnp.exp(sbuf[c] - m)
        sbuf[c] = e
        return l + jnp.sum(e, axis=0, keepdims=True)

    inv_l = 1.0 / lax.fori_loop(kb0, win, exp_step, l0)

    def grad_step(c, carry):
        p = sbuf[c] * inv_l
        vc = kvbuf[s, c, :, width:]
        dpt = lax.dot_general(vc, doall[...], nt, preferred_element_type=jnp.float32)
        ds = (p * (dpt - delta)).astype(jnp.bfloat16)
        pb = p.astype(jnp.bfloat16)
        dk = jnp.dot(ds, qall[...], preferred_element_type=jnp.float32) * scaling
        dv = jnp.dot(pb, doall[...], preferred_element_type=jnp.float32)
        dst = dst_ref[s * win + c]
        part_ref[dst, :, :width] += dk
        part_ref[dst, :, width:] += dv
        dsbuf[c] = ds
        return carry

    lax.fori_loop(kb0, win, grad_step, 0)

    def clear_step(c, carry):
        dsbuf[c] = jnp.zeros((rows, cols), jnp.bfloat16)
        return carry

    lax.fori_loop(0, kb0, clear_step, 0)
    kwin = kvbuf[s, :, :, :width].reshape(win * rows, width)
    dqt[...] = lax.dot_general(
        kwin, dsbuf[...].reshape(win * rows, cols), tn, preferred_element_type=jnp.float32
    )
    for h in range(heads):
        piece = dqt[:, h * rows:(h + 1) * rows]
        dq_ref[:, h * width:(h + 1) * width] = (piece.T * scaling).astype(jnp.bfloat16)


def _shift(x, k, n, axis):
    return lax.ppermute(x, axis, [(i, (i + k) % n) for i in range(n)])


def _group_gather(x, n, axis):
    return jnp.stack([x] + [_shift(x, k, n, axis) for k in range(1, n)])


def _group_reduce(parts, n, axis, dim):
    me = lax.axis_index(axis)
    total = lax.dynamic_index_in_dim(parts, me, dim, keepdims=False).astype(jnp.float32)
    for k in range(1, n):
        piece = lax.dynamic_index_in_dim(parts, (me + k) % n, dim, keepdims=False)
        total = total + _shift(piece.astype(jnp.bfloat16), k, n, axis).astype(jnp.float32)
    return total


def body(queries, shared_keys, shared_values, outputs, out_grad, doc_lengths):
    n_in = lax.axis_size("w")
    rank = lax.axis_index("zp") * n_in + lax.axis_index("w")
    n_out = lax.axis_size("zp")
    n_seq = n_out * n_in
    rows = shared_keys.shape[0] // 2
    width = shared_keys.shape[1]
    heads = queries.shape[1] // width
    scaling = width ** (-0.5)
    win = REACH + 1
    doc_ends = jnp.cumsum(doc_lengths)
    doc_starts = doc_ends - doc_lengths
    blocks = jnp.stack([rank, 2 * n_seq - 1 - rank]).astype(jnp.int32)

    kv_local = jnp.concatenate([shared_keys, shared_values], axis=1)
    kv_col = _group_gather(kv_local, n_out, "zp")
    kv_pieces = [kv_col.reshape(n_out * 2 * rows, 2 * width)] + [
        _shift(kv_col, k, n_in, "w").reshape(n_out * 2 * rows, 2 * width) for k in range(1, n_in)
    ]

    me_z = lax.axis_index("zp")
    me_w = lax.axis_index("w")
    seq_blk = (blocks[:, None] - REACH + jnp.arange(win, dtype=jnp.int32)[None, :]).reshape(-1)
    seq_blk = jnp.maximum(seq_blk, 0)
    dev = jnp.where(seq_blk < n_seq, seq_blk, 2 * n_seq - 1 - seq_blk)
    slot = (seq_blk >= n_seq).astype(jnp.int32)
    k_z = (me_z - dev // n_in) % n_out
    k_w = (me_w - dev % n_in) % n_in
    srow = ((k_z * 2 + slot) * rows).astype(jnp.int32)
    src_piece = k_w.astype(jnp.int32)
    dst = (dev * 2 + slot).astype(jnp.int32)

    prod = out_grad.astype(jnp.float32) * outputs.astype(jnp.float32)
    deltas = jnp.sum(prod.reshape(2, rows, heads, width), axis=3)
    delta_t = jnp.swapaxes(deltas, 1, 2).reshape(2, 1, heads * rows)

    kernel = functools.partial(
        _bwd_kernel, rows=rows, heads=heads, width=width, reach=REACH, scaling=scaling,
        docs=doc_lengths.shape[0], pieces=n_in,
    )
    cols = heads * rows
    vec = pl.BlockSpec((None, 1, cols), lambda s, *_: (s, 0, 0))
    grid_spec = pltpu.PrefetchScalarGridSpec(
        num_scalar_prefetch=5,
        grid=(2,),
        in_specs=[
            pl.BlockSpec((rows, cols), lambda s, *_: (s, 0)),
            pl.BlockSpec((rows, cols), lambda s, *_: (s, 0)),
        ] + [pl.BlockSpec(memory_space=pl.ANY)] * n_in + [
            vec,
        ],
        out_specs=[
            pl.BlockSpec((rows, cols), lambda s, *_: (s, 0)),
            pl.BlockSpec((2 * n_seq, rows, 2 * width), lambda s, *_: (0, 0, 0)),
        ],
        scratch_shapes=[
            pltpu.VMEM((cols, width), jnp.bfloat16),
            pltpu.VMEM((cols, width), jnp.bfloat16),
            pltpu.VMEM((width, cols), jnp.float32),
            pltpu.VMEM((2, win, rows, 2 * width), jnp.bfloat16),
            pltpu.SemaphoreType.DMA((2, win)),
            pltpu.VMEM((win, rows, cols), jnp.float32),
            pltpu.VMEM((win, rows, cols), jnp.bfloat16),
        ],
    )
    flops = 2 * 2 * win * 6 * rows * cols * width
    grad_queries, partial = pl.pallas_call(
        kernel,
        grid_spec=grid_spec,
        out_shape=[
            jax.ShapeDtypeStruct((2 * rows, cols), jnp.bfloat16),
            jax.ShapeDtypeStruct((2 * n_seq, rows, 2 * width), jnp.float32),
        ],
        compiler_params=pltpu.CompilerParams(dimension_semantics=("arbitrary",)),
        cost_estimate=pl.CostEstimate(
            flops=flops, transcendentals=2 * 2 * win * rows * cols, bytes_accessed=8 << 20
        ),
    )(blocks, doc_starts.astype(jnp.int32), srow, src_piece, dst, queries, out_grad,
      *kv_pieces, delta_t)

    storage = partial
    storage = storage.reshape(n_out, n_in, 2, rows, 2 * width)
    plane = _group_reduce(storage, n_in, "w", 1)
    summed = _group_reduce(plane, n_out, "zp", 0).reshape(2 * rows, 2 * width)
    grad_keys = summed[:, :width].astype(jnp.bfloat16)
    grad_values = summed[:, width:].astype(jnp.bfloat16)
    return (grad_queries, grad_keys, grad_values)


GROUP = 4


def solution(mesh):
    n_seq, n_grp = mesh.devices.shape
    split = mesh.devices.reshape(n_seq // GROUP, GROUP, n_grp)
    mesh2 = jax.sharding.Mesh(split, ("zp", "w", "grp"))
    rows = P(("zp", "w"), "grp")
    placed = (rows, rows, rows, rows, rows, P())
    return jax.shard_map(
        body,
        mesh=mesh2,
        in_specs=placed,
        out_specs=(rows, rows, rows),
        check_vma=False,
    )
```

```python
import functools

import jax
import numpy as np
import jax.numpy as jnp
from jax import lax
from jax.experimental import pallas as pl
from jax.experimental.pallas import tpu as pltpu
from jax.sharding import PartitionSpec as P

REACH = 16


def _bwd_kernel(blk_ref, starts_ref, srow_ref, src_ref, dst_ref, q_ref, do_ref, *rest,
                rows, heads, width, reach, scaling, docs, pieces):
    kv_refs = rest[:pieces]
    (delta_ref, dq_ref, part_ref, qall, doall, dqt, kvbuf, sems, sbuf, dsbuf) = rest[pieces:]
    s = pl.program_id(0)
    win = reach + 1

    def copy(side, i, ref):
        row = pl.multiple_of(srow_ref[side * win + i], rows)
        return pltpu.make_async_copy(
            ref.at[pl.ds(row, rows)], kvbuf.at[side, i], sems.at[side, i]
        )

    @pl.when(s == 0)
    def _():
        for side in range(2):
            for i in range(win):
                which = src_ref[side * win + i]
                for t in range(pieces):
                    @pl.when(which == t)
                    def _():
                        copy(side, i, kv_refs[t]).start()
        part_ref[...] = jnp.zeros(part_ref.shape, jnp.float32)

    b = blk_ref[s]
    cols = heads * rows
    qpos = b * rows + lax.broadcasted_iota(jnp.int32, (1, cols), 1) % rows
    first = b * rows

    def doc_step(j, carry):
        vec, low = carry
        st = starts_ref[j]
        vec = jnp.where(st <= qpos, jnp.maximum(vec, st), vec)
        low = jnp.where(st <= first, jnp.maximum(low, st), low)
        return vec, low

    begin, low = lax.fori_loop(
        0, docs, doc_step, (jnp.zeros((1, cols), jnp.int32), jnp.int32(0))
    )
    kb0 = jnp.maximum(0, low // rows - (b - reach))
    for h in range(heads):
        qall[h * rows:(h + 1) * rows, :] = q_ref[:, h * width:(h + 1) * width]
        doall[h * rows:(h + 1) * rows, :] = do_ref[:, h * width:(h + 1) * width]
    delta = delta_ref[...]
    k_iota = lax.broadcasted_iota(jnp.int32, (rows, 1), 0)
    base = (b - reach) * rows
    nt = (((1,), (1,)), ((), ()))
    tn = (((0,), (0,)), ((), ()))
    for i in range(win):
        copy(s, i, kv_refs[0]).wait()

    def scores(c):
        kc = kvbuf[s, c, :, :width]
        st = lax.dot_general(kc, qall[...], nt, preferred_element_type=jnp.float32) * scaling
        kpos = base + c * rows + k_iota
        allowed = (kpos >= begin) & (kpos <= qpos)
        return kc, st, allowed

    def stat_step(c, m):
        _, st, allowed = scores(c)
        masked = jnp.where(allowed, st, -1e30)
        sbuf[c] = masked
        return jnp.maximum(m, jnp.max(masked, axis=0, keepdims=True))

    m0 = jnp.full((1, cols), -1e30, jnp.float32)
    l0 = jnp.zeros((1, cols), jnp.float32)
    m = lax.fori_loop(kb0, win, stat_step, m0)

    def exp_step(c, l):
        e = jnp.exp(sbuf[c] - m)
        sbuf[c] = e
        return l + jnp.sum(e, axis=0, keepdims=True)

    inv_l = 1.0 / lax.fori_loop(kb0, win, exp_step, l0)

    def grad_step(c, carry):
        p = sbuf[c] * inv_l
        vc = kvbuf[s, c, :, width:]
        dpt = lax.dot_general(vc, doall[...], nt, preferred_element_type=jnp.float32)
        ds = (p * (dpt - delta)).astype(jnp.bfloat16)
        pb = p.astype(jnp.bfloat16)
        dk = jnp.dot(ds, qall[...], preferred_element_type=jnp.float32) * scaling
        dv = jnp.dot(pb, doall[...], preferred_element_type=jnp.float32)
        dst = dst_ref[s * win + c]
        part_ref[dst, :, :width] += dk
        part_ref[dst, :, width:] += dv
        dsbuf[c] = ds
        return carry

    lax.fori_loop(kb0, win, grad_step, 0)

    def clear_step(c, carry):
        dsbuf[c] = jnp.zeros((rows, cols), jnp.bfloat16)
        return carry

    lax.fori_loop(0, kb0, clear_step, 0)
    kwin = kvbuf[s, :, :, :width].reshape(win * rows, width)
    dqt[...] = lax.dot_general(
        kwin, dsbuf[...].reshape(win * rows, cols), tn, preferred_element_type=jnp.float32
    )
    for h in range(heads):
        piece = dqt[:, h * rows:(h + 1) * rows]
        dq_ref[:, h * width:(h + 1) * width] = (piece.T * scaling).astype(jnp.bfloat16)


def _plane_tables(n_seq, n_out, n_in, reach):
    def needs(dp, d, slot):
        j = d if slot == 0 else 2 * n_seq - 1 - d
        up = 2 * n_seq - 1 - dp
        return (dp - reach <= j <= dp) or (up - reach <= j <= up)

    lists = {}
    for sr in range(n_seq):
        zs, ws = divmod(sr, n_in)
        for k in range(1, n_in):
            rr = zs * n_in + (ws + k) % n_in
            got = []
            for e in range(2 * n_out):
                kz, slot = divmod(e, 2)
                d = ((zs - kz) % n_out) * n_in + ws
                if needs(rr, d, slot):
                    got.append(e)
            lists[sr, k] = got
    most = max(len(v) for v in lists.values())
    send = np.zeros((n_seq, n_in - 1, most), np.int32)
    where = np.zeros((n_seq, n_in - 1, 2 * n_out), np.int32)
    for (sr, k), got in lists.items():
        padded = got + [got[0] if got else 0] * (most - len(got))
        send[sr, k - 1] = padded
        for i, e in enumerate(got):
            where[sr, k - 1, e] = i
    return most, send, where


def _shift(x, k, n, axis):
    return lax.ppermute(x, axis, [(i, (i + k) % n) for i in range(n)])


def _group_gather(x, n, axis):
    return jnp.stack([x] + [_shift(x, k, n, axis) for k in range(1, n)])


def _group_reduce(parts, n, axis, dim):
    me = lax.axis_index(axis)
    total = lax.dynamic_index_in_dim(parts, me, dim, keepdims=False).astype(jnp.float32)
    for k in range(1, n):
        piece = lax.dynamic_index_in_dim(parts, (me + k) % n, dim, keepdims=False)
        total = total + _shift(piece.astype(jnp.bfloat16), k, n, axis).astype(jnp.float32)
    return total


def body(queries, shared_keys, shared_values, outputs, out_grad, doc_lengths):
    n_in = lax.axis_size("w")
    rank = lax.axis_index("zp") * n_in + lax.axis_index("w")
    n_out = lax.axis_size("zp")
    n_seq = n_out * n_in
    rows = shared_keys.shape[0] // 2
    width = shared_keys.shape[1]
    heads = queries.shape[1] // width
    scaling = width ** (-0.5)
    win = REACH + 1
    doc_ends = jnp.cumsum(doc_lengths)
    doc_starts = doc_ends - doc_lengths
    blocks = jnp.stack([rank, 2 * n_seq - 1 - rank]).astype(jnp.int32)

    kv_local = jnp.concatenate([shared_keys, shared_values], axis=1)
    kv_col = _group_gather(kv_local, n_out, "zp")
    most, send_np, where_np = _plane_tables(n_seq, n_out, n_in, REACH)
    send_tab = jnp.asarray(send_np)[rank]
    entries = kv_col.reshape(n_out * 2, rows, 2 * width)
    kv_pieces = [kv_col.reshape(n_out * 2 * rows, 2 * width)]
    for k in range(1, n_in):
        chosen = jnp.take(entries, send_tab[k - 1], axis=0)
        kv_pieces.append(_shift(chosen, k, n_in, "w").reshape(most * rows, 2 * width))

    me_z = lax.axis_index("zp")
    me_w = lax.axis_index("w")
    seq_blk = (blocks[:, None] - REACH + jnp.arange(win, dtype=jnp.int32)[None, :]).reshape(-1)
    seq_blk = jnp.maximum(seq_blk, 0)
    dev = jnp.where(seq_blk < n_seq, seq_blk, 2 * n_seq - 1 - seq_blk)
    slot = (seq_blk >= n_seq).astype(jnp.int32)
    k_z = (me_z - dev // n_in) % n_out
    k_w = (me_w - dev % n_in) % n_in
    entry = k_z * 2 + slot
    sender = me_z * n_in + dev % n_in
    pos = jnp.asarray(where_np)[sender, jnp.maximum(k_w - 1, 0), entry]
    srow = (jnp.where(k_w == 0, entry, pos) * rows).astype(jnp.int32)
    src_piece = k_w.astype(jnp.int32)
    dst = (dev * 2 + slot).astype(jnp.int32)

    prod = out_grad.astype(jnp.float32) * outputs.astype(jnp.float32)
    deltas = jnp.sum(prod.reshape(2, rows, heads, width), axis=3)
    delta_t = jnp.swapaxes(deltas, 1, 2).reshape(2, 1, heads * rows)

    kernel = functools.partial(
        _bwd_kernel, rows=rows, heads=heads, width=width, reach=REACH, scaling=scaling,
        docs=doc_lengths.shape[0], pieces=n_in,
    )
    cols = heads * rows
    vec = pl.BlockSpec((None, 1, cols), lambda s, *_: (s, 0, 0))
    grid_spec = pltpu.PrefetchScalarGridSpec(
        num_scalar_prefetch=5,
        grid=(2,),
        in_specs=[
            pl.BlockSpec((rows, cols), lambda s, *_: (s, 0)),
            pl.BlockSpec((rows, cols), lambda s, *_: (s, 0)),
        ] + [pl.BlockSpec(memory_space=pl.ANY)] * n_in + [
            vec,
        ],
        out_specs=[
            pl.BlockSpec((rows, cols), lambda s, *_: (s, 0)),
            pl.BlockSpec((2 * n_seq, rows, 2 * width), lambda s, *_: (0, 0, 0)),
        ],
        scratch_shapes=[
            pltpu.VMEM((cols, width), jnp.bfloat16),
            pltpu.VMEM((cols, width), jnp.bfloat16),
            pltpu.VMEM((width, cols), jnp.float32),
            pltpu.VMEM((2, win, rows, 2 * width), jnp.bfloat16),
            pltpu.SemaphoreType.DMA((2, win)),
            pltpu.VMEM((win, rows, cols), jnp.float32),
            pltpu.VMEM((win, rows, cols), jnp.bfloat16),
        ],
    )
    flops = 2 * 2 * win * 6 * rows * cols * width
    grad_queries, partial = pl.pallas_call(
        kernel,
        grid_spec=grid_spec,
        out_shape=[
            jax.ShapeDtypeStruct((2 * rows, cols), jnp.bfloat16),
            jax.ShapeDtypeStruct((2 * n_seq, rows, 2 * width), jnp.float32),
        ],
        compiler_params=pltpu.CompilerParams(dimension_semantics=("arbitrary",)),
        cost_estimate=pl.CostEstimate(
            flops=flops, transcendentals=2 * 2 * win * rows * cols, bytes_accessed=8 << 20
        ),
    )(blocks, doc_starts.astype(jnp.int32), srow, src_piece, dst, queries, out_grad,
      *kv_pieces, delta_t)

    storage = partial
    storage = storage.reshape(n_out, n_in, 2, rows, 2 * width)
    plane = _group_reduce(storage, n_in, "w", 1)
    summed = _group_reduce(plane, n_out, "zp", 0).reshape(2 * rows, 2 * width)
    grad_keys = summed[:, :width].astype(jnp.bfloat16)
    grad_values = summed[:, width:].astype(jnp.bfloat16)
    return (grad_queries, grad_keys, grad_values)


GROUP = 4


def solution(mesh):
    n_seq, n_grp = mesh.devices.shape
    split = mesh.devices.reshape(n_seq // GROUP, GROUP, n_grp)
    mesh2 = jax.sharding.Mesh(split, ("zp", "w", "grp"))
    rows = P(("zp", "w"), "grp")
    placed = (rows, rows, rows, rows, rows, P())
    return jax.shard_map(
        body,
        mesh=mesh2,
        in_specs=placed,
        out_specs=(rows, rows, rows),
        check_vma=False,
    )
```

```python
import functools

import jax
import numpy as np
import jax.numpy as jnp
from jax import lax
from jax.experimental import pallas as pl
from jax.experimental.pallas import tpu as pltpu
from jax.sharding import PartitionSpec as P

REACH = 16


def _bwd_kernel(blk_ref, starts_ref, srow_ref, src_ref, dst_ref, q_ref, do_ref, *rest,
                rows, heads, width, reach, scaling, docs, pieces):
    kv_refs = rest[:pieces]
    (delta_ref, dq_ref, part_ref, qall, doall, dqt, kvbuf, sems, sbuf, dsbuf) = rest[pieces:]
    s = pl.program_id(0)
    win = reach + 1

    def copy(side, i, ref):
        row = pl.multiple_of(srow_ref[side * win + i], rows)
        return pltpu.make_async_copy(
            ref.at[pl.ds(row, rows)], kvbuf.at[side, i], sems.at[side, i]
        )

    @pl.when(s == 0)
    def _():
        for side in range(2):
            for i in range(win):
                which = src_ref[side * win + i]
                for t in range(pieces):
                    @pl.when(which == t)
                    def _():
                        copy(side, i, kv_refs[t]).start()
        part_ref[...] = jnp.zeros(part_ref.shape, jnp.float32)

    b = blk_ref[s]
    cols = heads * rows
    qpos = b * rows + lax.broadcasted_iota(jnp.int32, (1, cols), 1) % rows
    first = b * rows

    def doc_step(j, carry):
        vec, low = carry
        st = starts_ref[j]
        vec = jnp.where(st <= qpos, jnp.maximum(vec, st), vec)
        low = jnp.where(st <= first, jnp.maximum(low, st), low)
        return vec, low

    begin, low = lax.fori_loop(
        0, docs, doc_step, (jnp.zeros((1, cols), jnp.int32), jnp.int32(0))
    )
    kb0 = jnp.maximum(0, low // rows - (b - reach))
    for h in range(heads):
        qall[h * rows:(h + 1) * rows, :] = q_ref[:, h * width:(h + 1) * width]
        doall[h * rows:(h + 1) * rows, :] = do_ref[:, h * width:(h + 1) * width]
    delta = delta_ref[...]
    k_iota = lax.broadcasted_iota(jnp.int32, (rows, 1), 0)
    base = (b - reach) * rows
    nt = (((1,), (1,)), ((), ()))
    tn = (((0,), (0,)), ((), ()))
    for i in range(win):
        copy(s, i, kv_refs[0]).wait()

    def scores(c):
        kc = kvbuf[s, c, :, :width]
        st = lax.dot_general(kc, qall[...], nt, preferred_element_type=jnp.float32) * scaling
        kpos = base + c * rows + k_iota
        allowed = (kpos >= begin) & (kpos <= qpos)
        return kc, st, allowed

    def stat_step(c, m):
        _, st, allowed = scores(c)
        masked = jnp.where(allowed, st, -1e30)
        sbuf[c] = masked
        return jnp.maximum(m, jnp.max(masked, axis=0, keepdims=True))

    m0 = jnp.full((1, cols), -1e30, jnp.float32)
    l0 = jnp.zeros((1, cols), jnp.float32)
    m = lax.fori_loop(kb0, win, stat_step, m0)

    def exp_step(c, l):
        e = jnp.exp(sbuf[c] - m)
        sbuf[c] = e
        return l + jnp.sum(e, axis=0, keepdims=True)

    inv_l = 1.0 / lax.fori_loop(kb0, win, exp_step, l0)

    def grad_step(c, carry):
        p = sbuf[c] * inv_l
        vc = kvbuf[s, c, :, width:]
        dpt = lax.dot_general(vc, doall[...], nt, preferred_element_type=jnp.float32)
        ds = (p * (dpt - delta)).astype(jnp.bfloat16)
        pb = p.astype(jnp.bfloat16)
        dk = jnp.dot(ds, qall[...], preferred_element_type=jnp.float32) * scaling
        dv = jnp.dot(pb, doall[...], preferred_element_type=jnp.float32)
        dst = dst_ref[s * win + c]
        part_ref[dst, :, :width] += dk
        part_ref[dst, :, width:] += dv
        dsbuf[c] = ds
        return carry

    lax.fori_loop(kb0, win, grad_step, 0)

    def clear_step(c, carry):
        dsbuf[c] = jnp.zeros((rows, cols), jnp.bfloat16)
        return carry

    lax.fori_loop(0, kb0, clear_step, 0)
    kwin = kvbuf[s, :, :, :width].reshape(win * rows, width)
    dqt[...] = lax.dot_general(
        kwin, dsbuf[...].reshape(win * rows, cols), tn, preferred_element_type=jnp.float32
    )
    for h in range(heads):
        piece = dqt[:, h * rows:(h + 1) * rows]
        dq_ref[:, h * width:(h + 1) * width] = (piece.T * scaling).astype(jnp.bfloat16)


def _plane_tables(n_seq, n_out, n_in, reach):
    def needs(dp, d, slot):
        j = d if slot == 0 else 2 * n_seq - 1 - d
        up = 2 * n_seq - 1 - dp
        return (dp - reach <= j <= dp) or (up - reach <= j <= up)

    lists = {}
    for sr in range(n_seq):
        zs, ws = divmod(sr, n_in)
        for k in range(1, n_in):
            rr = zs * n_in + (ws + k) % n_in
            got = []
            for e in range(2 * n_out):
                kz, slot = divmod(e, 2)
                d = ((zs - kz) % n_out) * n_in + ws
                if needs(rr, d, slot):
                    got.append(e)
            lists[sr, k] = got
    most = max(len(v) for v in lists.values())
    send = np.zeros((n_seq, n_in - 1, most), np.int32)
    where = np.zeros((n_seq, n_in - 1, 2 * n_out), np.int32)
    for (sr, k), got in lists.items():
        padded = got + [got[0] if got else 0] * (most - len(got))
        send[sr, k - 1] = padded
        for i, e in enumerate(got):
            where[sr, k - 1, e] = i
    return most, send, where


def _partial_tables(n_seq, n_out, n_in, reach):
    def needs(dp, d, slot):
        j = d if slot == 0 else 2 * n_seq - 1 - d
        up = 2 * n_seq - 1 - dp
        return (dp - reach <= j <= dp) or (up - reach <= j <= up)

    lists = {}
    for sr in range(n_seq):
        zs, ws = divmod(sr, n_in)
        for k in range(1, n_in):
            wr = (ws + k) % n_in
            lists[sr, k] = [
                e for e in range(2 * n_out) if needs(sr, (e // 2) * n_in + wr, e % 2)
            ]
    most = max(len(v) for v in lists.values())
    send = np.zeros((n_seq, n_in - 1, most), np.int32)
    where = np.full((n_seq, n_in - 1, 2 * n_out), -1, np.int32)
    for (sr, k), got in lists.items():
        send[sr, k - 1] = got + [got[0] if got else 0] * (most - len(got))
        for i, e in enumerate(got):
            where[sr, k - 1, e] = i
    return most, send, where


def _plane_reduce(storage, rank, n_seq, n_out, n_in, reach):
    most, send_np, where_np = _partial_tables(n_seq, n_out, n_in, reach)
    me_w = lax.axis_index("w")
    me_z = lax.axis_index("zp")
    send_tab = jnp.asarray(send_np)[rank]
    where_tab = jnp.asarray(where_np)
    block = storage.shape[3:]
    total = lax.dynamic_index_in_dim(storage, me_w, 1, keepdims=False)
    total = total.reshape((2 * n_out,) + block)
    for k in range(1, n_in):
        piece = lax.dynamic_index_in_dim(storage, (me_w + k) % n_in, 1, keepdims=False)
        piece = piece.reshape((2 * n_out,) + block)
        chosen = jnp.take(piece, send_tab[k - 1], axis=0).astype(jnp.bfloat16)
        got = _shift(chosen, k, n_in, "w")
        sender = me_z * n_in + (me_w - k) % n_in
        pos = where_tab[sender, k - 1]
        picked = jnp.take(got, jnp.maximum(pos, 0), axis=0).astype(jnp.float32)
        total = total + jnp.where((pos >= 0)[:, None, None], picked, 0.0)
    return total.reshape((n_out, 2) + block)


def _shift(x, k, n, axis):
    return lax.ppermute(x, axis, [(i, (i + k) % n) for i in range(n)])


def _group_gather(x, n, axis):
    return jnp.stack([x] + [_shift(x, k, n, axis) for k in range(1, n)])


def _group_reduce(parts, n, axis, dim):
    me = lax.axis_index(axis)
    total = lax.dynamic_index_in_dim(parts, me, dim, keepdims=False).astype(jnp.float32)
    for k in range(1, n):
        piece = lax.dynamic_index_in_dim(parts, (me + k) % n, dim, keepdims=False)
        total = total + _shift(piece.astype(jnp.bfloat16), k, n, axis).astype(jnp.float32)
    return total


def body(queries, shared_keys, shared_values, outputs, out_grad, doc_lengths):
    n_in = lax.axis_size("w")
    rank = lax.axis_index("zp") * n_in + lax.axis_index("w")
    n_out = lax.axis_size("zp")
    n_seq = n_out * n_in
    rows = shared_keys.shape[0] // 2
    width = shared_keys.shape[1]
    heads = queries.shape[1] // width
    scaling = width ** (-0.5)
    win = REACH + 1
    doc_ends = jnp.cumsum(doc_lengths)
    doc_starts = doc_ends - doc_lengths
    blocks = jnp.stack([rank, 2 * n_seq - 1 - rank]).astype(jnp.int32)

    kv_local = jnp.concatenate([shared_keys, shared_values], axis=1)
    kv_col = _group_gather(kv_local, n_out, "zp")
    most, send_np, where_np = _plane_tables(n_seq, n_out, n_in, REACH)
    send_tab = jnp.asarray(send_np)[rank]
    entries = kv_col.reshape(n_out * 2, rows, 2 * width)
    kv_pieces = [kv_col.reshape(n_out * 2 * rows, 2 * width)]
    for k in range(1, n_in):
        chosen = jnp.take(entries, send_tab[k - 1], axis=0)
        kv_pieces.append(_shift(chosen, k, n_in, "w").reshape(most * rows, 2 * width))

    me_z = lax.axis_index("zp")
    me_w = lax.axis_index("w")
    seq_blk = (blocks[:, None] - REACH + jnp.arange(win, dtype=jnp.int32)[None, :]).reshape(-1)
    seq_blk = jnp.maximum(seq_blk, 0)
    dev = jnp.where(seq_blk < n_seq, seq_blk, 2 * n_seq - 1 - seq_blk)
    slot = (seq_blk >= n_seq).astype(jnp.int32)
    k_z = (me_z - dev // n_in) % n_out
    k_w = (me_w - dev % n_in) % n_in
    entry = k_z * 2 + slot
    sender = me_z * n_in + dev % n_in
    pos = jnp.asarray(where_np)[sender, jnp.maximum(k_w - 1, 0), entry]
    srow = (jnp.where(k_w == 0, entry, pos) * rows).astype(jnp.int32)
    src_piece = k_w.astype(jnp.int32)
    dst = (dev * 2 + slot).astype(jnp.int32)

    prod = out_grad.astype(jnp.float32) * outputs.astype(jnp.float32)
    deltas = jnp.sum(prod.reshape(2, rows, heads, width), axis=3)
    delta_t = jnp.swapaxes(deltas, 1, 2).reshape(2, 1, heads * rows)

    kernel = functools.partial(
        _bwd_kernel, rows=rows, heads=heads, width=width, reach=REACH, scaling=scaling,
        docs=doc_lengths.shape[0], pieces=n_in,
    )
    cols = heads * rows
    vec = pl.BlockSpec((None, 1, cols), lambda s, *_: (s, 0, 0))
    grid_spec = pltpu.PrefetchScalarGridSpec(
        num_scalar_prefetch=5,
        grid=(2,),
        in_specs=[
            pl.BlockSpec((rows, cols), lambda s, *_: (s, 0)),
            pl.BlockSpec((rows, cols), lambda s, *_: (s, 0)),
        ] + [pl.BlockSpec(memory_space=pl.ANY)] * n_in + [
            vec,
        ],
        out_specs=[
            pl.BlockSpec((rows, cols), lambda s, *_: (s, 0)),
            pl.BlockSpec((2 * n_seq, rows, 2 * width), lambda s, *_: (0, 0, 0)),
        ],
        scratch_shapes=[
            pltpu.VMEM((cols, width), jnp.bfloat16),
            pltpu.VMEM((cols, width), jnp.bfloat16),
            pltpu.VMEM((width, cols), jnp.float32),
            pltpu.VMEM((2, win, rows, 2 * width), jnp.bfloat16),
            pltpu.SemaphoreType.DMA((2, win)),
            pltpu.VMEM((win, rows, cols), jnp.float32),
            pltpu.VMEM((win, rows, cols), jnp.bfloat16),
        ],
    )
    flops = 2 * 2 * win * 6 * rows * cols * width
    grad_queries, partial = pl.pallas_call(
        kernel,
        grid_spec=grid_spec,
        out_shape=[
            jax.ShapeDtypeStruct((2 * rows, cols), jnp.bfloat16),
            jax.ShapeDtypeStruct((2 * n_seq, rows, 2 * width), jnp.float32),
        ],
        compiler_params=pltpu.CompilerParams(dimension_semantics=("arbitrary",)),
        cost_estimate=pl.CostEstimate(
            flops=flops, transcendentals=2 * 2 * win * rows * cols, bytes_accessed=8 << 20
        ),
    )(blocks, doc_starts.astype(jnp.int32), srow, src_piece, dst, queries, out_grad,
      *kv_pieces, delta_t)

    storage = partial
    storage = storage.reshape(n_out, n_in, 2, rows, 2 * width)
    plane = _plane_reduce(storage, rank, n_seq, n_out, n_in, REACH)
    summed = _group_reduce(plane, n_out, "zp", 0).reshape(2 * rows, 2 * width)
    grad_keys = summed[:, :width].astype(jnp.bfloat16)
    grad_values = summed[:, width:].astype(jnp.bfloat16)
    return (grad_queries, grad_keys, grad_values)


GROUP = 4


def solution(mesh):
    n_seq, n_grp = mesh.devices.shape
    split = mesh.devices.reshape(n_seq // GROUP, GROUP, n_grp)
    mesh2 = jax.sharding.Mesh(split, ("zp", "w", "grp"))
    rows = P(("zp", "w"), "grp")
    placed = (rows, rows, rows, rows, rows, P())
    return jax.shard_map(
        body,
        mesh=mesh2,
        in_specs=placed,
        out_specs=(rows, rows, rows),
        check_vma=False,
    )
```

```python
import functools

import jax
import numpy as np
import jax.numpy as jnp
from jax import lax
from jax.experimental import pallas as pl
from jax.experimental.pallas import tpu as pltpu
from jax.sharding import PartitionSpec as P

REACH = 16


def _bwd_kernel(blk_ref, starts_ref, srow_ref, src_ref, dst_ref, q_ref, do_ref, *rest,
                rows, heads, width, reach, scaling, docs, pieces):
    kv_refs = rest[:pieces]
    (delta_ref, dq_ref, part_ref, qall, doall, dqt, kvbuf, sems, sbuf, dsbuf, qt,
     dot_t) = rest[pieces:]
    s = pl.program_id(0)
    win = reach + 1

    def copy(side, i, ref):
        row = pl.multiple_of(srow_ref[side * win + i], rows)
        return pltpu.make_async_copy(
            ref.at[pl.ds(row, rows)], kvbuf.at[side, i], sems.at[side, i]
        )

    @pl.when(s == 0)
    def _():
        for side in range(2):
            for i in range(win):
                which = src_ref[side * win + i]
                for t in range(pieces):
                    @pl.when(which == t)
                    def _():
                        copy(side, i, kv_refs[t]).start()
        part_ref[...] = jnp.zeros(part_ref.shape, jnp.float32)

    b = blk_ref[s]
    cols = heads * rows
    qpos = b * rows + lax.broadcasted_iota(jnp.int32, (1, cols), 1) % rows
    first = b * rows

    def doc_step(j, carry):
        vec, low = carry
        st = starts_ref[j]
        vec = jnp.where(st <= qpos, jnp.maximum(vec, st), vec)
        low = jnp.where(st <= first, jnp.maximum(low, st), low)
        return vec, low

    begin, low = lax.fori_loop(
        0, docs, doc_step, (jnp.zeros((1, cols), jnp.int32), jnp.int32(0))
    )
    kb0 = jnp.maximum(0, low // rows - (b - reach))
    for h in range(heads):
        q_h = q_ref[:, h * width:(h + 1) * width]
        do_h = do_ref[:, h * width:(h + 1) * width]
        qall[h * rows:(h + 1) * rows, :] = q_h
        doall[h * rows:(h + 1) * rows, :] = do_h
        qt[:, h * rows:(h + 1) * rows] = q_h.astype(jnp.float32).T.astype(jnp.bfloat16)
        dot_t[:, h * rows:(h + 1) * rows] = do_h.astype(jnp.float32).T.astype(jnp.bfloat16)
    delta = delta_ref[...]
    k_iota = lax.broadcasted_iota(jnp.int32, (rows, 1), 0)
    base = (b - reach) * rows
    nt = (((1,), (1,)), ((), ()))
    tn = (((0,), (0,)), ((), ()))
    for i in range(win):
        copy(s, i, kv_refs[0]).wait()

    def scores(c):
        kc = kvbuf[s, c, :, :width]
        st = jnp.dot(kc, qt[...], preferred_element_type=jnp.float32) * scaling
        kpos = base + c * rows + k_iota
        allowed = (kpos >= begin) & (kpos <= qpos)
        return kc, st, allowed

    def stat_step(c, m):
        _, st, allowed = scores(c)
        masked = jnp.where(allowed, st, -1e30)
        sbuf[c] = masked
        return jnp.maximum(m, jnp.max(masked, axis=0, keepdims=True))

    m0 = jnp.full((1, cols), -1e30, jnp.float32)
    l0 = jnp.zeros((1, cols), jnp.float32)
    m = lax.fori_loop(kb0, win, stat_step, m0)

    def exp_step(c, l):
        e = jnp.exp(sbuf[c] - m)
        sbuf[c] = e
        return l + jnp.sum(e, axis=0, keepdims=True)

    inv_l = 1.0 / lax.fori_loop(kb0, win, exp_step, l0)

    def grad_step(c, carry):
        p = sbuf[c] * inv_l
        vc = kvbuf[s, c, :, width:]
        dpt = jnp.dot(vc, dot_t[...], preferred_element_type=jnp.float32)
        ds = (p * (dpt - delta)).astype(jnp.bfloat16)
        pb = p.astype(jnp.bfloat16)
        dk = jnp.dot(ds, qall[...], preferred_element_type=jnp.float32) * scaling
        dv = jnp.dot(pb, doall[...], preferred_element_type=jnp.float32)
        dst = dst_ref[s * win + c]
        part_ref[dst, :, :width] += dk
        part_ref[dst, :, width:] += dv
        dsbuf[c] = ds
        return carry

    lax.fori_loop(kb0, win, grad_step, 0)

    def clear_step(c, carry):
        dsbuf[c] = jnp.zeros((rows, cols), jnp.bfloat16)
        return carry

    lax.fori_loop(0, kb0, clear_step, 0)
    kwin = kvbuf[s, :, :, :width].reshape(win * rows, width)
    dqt[...] = lax.dot_general(
        kwin, dsbuf[...].reshape(win * rows, cols), tn, preferred_element_type=jnp.float32
    )
    for h in range(heads):
        piece = dqt[:, h * rows:(h + 1) * rows]
        dq_ref[:, h * width:(h + 1) * width] = (piece.T * scaling).astype(jnp.bfloat16)


def _plane_tables(n_seq, n_out, n_in, reach):
    def needs(dp, d, slot):
        j = d if slot == 0 else 2 * n_seq - 1 - d
        up = 2 * n_seq - 1 - dp
        return (dp - reach <= j <= dp) or (up - reach <= j <= up)

    lists = {}
    for sr in range(n_seq):
        zs, ws = divmod(sr, n_in)
        for k in range(1, n_in):
            rr = zs * n_in + (ws + k) % n_in
            got = []
            for e in range(2 * n_out):
                kz, slot = divmod(e, 2)
                d = ((zs - kz) % n_out) * n_in + ws
                if needs(rr, d, slot):
                    got.append(e)
            lists[sr, k] = got
    most = max(len(v) for v in lists.values())
    send = np.zeros((n_seq, n_in - 1, most), np.int32)
    where = np.zeros((n_seq, n_in - 1, 2 * n_out), np.int32)
    for (sr, k), got in lists.items():
        padded = got + [got[0] if got else 0] * (most - len(got))
        send[sr, k - 1] = padded
        for i, e in enumerate(got):
            where[sr, k - 1, e] = i
    return most, send, where


def _partial_tables(n_seq, n_out, n_in, reach):
    def needs(dp, d, slot):
        j = d if slot == 0 else 2 * n_seq - 1 - d
        up = 2 * n_seq - 1 - dp
        return (dp - reach <= j <= dp) or (up - reach <= j <= up)

    lists = {}
    for sr in range(n_seq):
        zs, ws = divmod(sr, n_in)
        for k in range(1, n_in):
            wr = (ws + k) % n_in
            lists[sr, k] = [
                e for e in range(2 * n_out) if needs(sr, (e // 2) * n_in + wr, e % 2)
            ]
    most = max(len(v) for v in lists.values())
    send = np.zeros((n_seq, n_in - 1, most), np.int32)
    where = np.full((n_seq, n_in - 1, 2 * n_out), -1, np.int32)
    for (sr, k), got in lists.items():
        send[sr, k - 1] = got + [got[0] if got else 0] * (most - len(got))
        for i, e in enumerate(got):
            where[sr, k - 1, e] = i
    return most, send, where


def _plane_reduce(storage, rank, n_seq, n_out, n_in, reach):
    most, send_np, where_np = _partial_tables(n_seq, n_out, n_in, reach)
    me_w = lax.axis_index("w")
    me_z = lax.axis_index("zp")
    send_tab = jnp.asarray(send_np)[rank]
    where_tab = jnp.asarray(where_np)
    block = storage.shape[3:]
    total = lax.dynamic_index_in_dim(storage, me_w, 1, keepdims=False)
    total = total.reshape((2 * n_out,) + block)
    for k in range(1, n_in):
        piece = lax.dynamic_index_in_dim(storage, (me_w + k) % n_in, 1, keepdims=False)
        piece = piece.reshape((2 * n_out,) + block)
        chosen = jnp.take(piece, send_tab[k - 1], axis=0).astype(jnp.bfloat16)
        got = _shift(chosen, k, n_in, "w")
        sender = me_z * n_in + (me_w - k) % n_in
        pos = where_tab[sender, k - 1]
        picked = jnp.take(got, jnp.maximum(pos, 0), axis=0).astype(jnp.float32)
        total = total + jnp.where((pos >= 0)[:, None, None], picked, 0.0)
    return total.reshape((n_out, 2) + block)


def _shift(x, k, n, axis):
    return lax.ppermute(x, axis, [(i, (i + k) % n) for i in range(n)])


def _group_gather(x, n, axis):
    return jnp.stack([x] + [_shift(x, k, n, axis) for k in range(1, n)])


def _group_reduce(parts, n, axis, dim):
    me = lax.axis_index(axis)
    total = lax.dynamic_index_in_dim(parts, me, dim, keepdims=False).astype(jnp.float32)
    for k in range(1, n):
        piece = lax.dynamic_index_in_dim(parts, (me + k) % n, dim, keepdims=False)
        total = total + _shift(piece.astype(jnp.bfloat16), k, n, axis).astype(jnp.float32)
    return total


def body(queries, shared_keys, shared_values, outputs, out_grad, doc_lengths):
    n_in = lax.axis_size("w")
    rank = lax.axis_index("zp") * n_in + lax.axis_index("w")
    n_out = lax.axis_size("zp")
    n_seq = n_out * n_in
    rows = shared_keys.shape[0] // 2
    width = shared_keys.shape[1]
    heads = queries.shape[1] // width
    scaling = width ** (-0.5)
    win = REACH + 1
    doc_ends = jnp.cumsum(doc_lengths)
    doc_starts = doc_ends - doc_lengths
    blocks = jnp.stack([rank, 2 * n_seq - 1 - rank]).astype(jnp.int32)

    kv_local = jnp.concatenate([shared_keys, shared_values], axis=1)
    kv_col = _group_gather(kv_local, n_out, "zp")
    most, send_np, where_np = _plane_tables(n_seq, n_out, n_in, REACH)
    send_tab = jnp.asarray(send_np)[rank]
    entries = kv_col.reshape(n_out * 2, rows, 2 * width)
    kv_pieces = [kv_col.reshape(n_out * 2 * rows, 2 * width)]
    for k in range(1, n_in):
        chosen = jnp.take(entries, send_tab[k - 1], axis=0)
        kv_pieces.append(_shift(chosen, k, n_in, "w").reshape(most * rows, 2 * width))

    me_z = lax.axis_index("zp")
    me_w = lax.axis_index("w")
    seq_blk = (blocks[:, None] - REACH + jnp.arange(win, dtype=jnp.int32)[None, :]).reshape(-1)
    seq_blk = jnp.maximum(seq_blk, 0)
    dev = jnp.where(seq_blk < n_seq, seq_blk, 2 * n_seq - 1 - seq_blk)
    slot = (seq_blk >= n_seq).astype(jnp.int32)
    k_z = (me_z - dev // n_in) % n_out
    k_w = (me_w - dev % n_in) % n_in
    entry = k_z * 2 + slot
    sender = me_z * n_in + dev % n_in
    pos = jnp.asarray(where_np)[sender, jnp.maximum(k_w - 1, 0), entry]
    srow = (jnp.where(k_w == 0, entry, pos) * rows).astype(jnp.int32)
    src_piece = k_w.astype(jnp.int32)
    dst = (dev * 2 + slot).astype(jnp.int32)

    prod = out_grad.astype(jnp.float32) * outputs.astype(jnp.float32)
    deltas = jnp.sum(prod.reshape(2, rows, heads, width), axis=3)
    delta_t = jnp.swapaxes(deltas, 1, 2).reshape(2, 1, heads * rows)

    kernel = functools.partial(
        _bwd_kernel, rows=rows, heads=heads, width=width, reach=REACH, scaling=scaling,
        docs=doc_lengths.shape[0], pieces=n_in,
    )
    cols = heads * rows
    vec = pl.BlockSpec((None, 1, cols), lambda s, *_: (s, 0, 0))
    grid_spec = pltpu.PrefetchScalarGridSpec(
        num_scalar_prefetch=5,
        grid=(2,),
        in_specs=[
            pl.BlockSpec((rows, cols), lambda s, *_: (s, 0)),
            pl.BlockSpec((rows, cols), lambda s, *_: (s, 0)),
        ] + [pl.BlockSpec(memory_space=pl.ANY)] * n_in + [
            vec,
        ],
        out_specs=[
            pl.BlockSpec((rows, cols), lambda s, *_: (s, 0)),
            pl.BlockSpec((2 * n_seq, rows, 2 * width), lambda s, *_: (0, 0, 0)),
        ],
        scratch_shapes=[
            pltpu.VMEM((cols, width), jnp.bfloat16),
            pltpu.VMEM((cols, width), jnp.bfloat16),
            pltpu.VMEM((width, cols), jnp.float32),
            pltpu.VMEM((2, win, rows, 2 * width), jnp.bfloat16),
            pltpu.SemaphoreType.DMA((2, win)),
            pltpu.VMEM((win, rows, cols), jnp.float32),
            pltpu.VMEM((win, rows, cols), jnp.bfloat16),
            pltpu.VMEM((width, cols), jnp.bfloat16),
            pltpu.VMEM((width, cols), jnp.bfloat16),
        ],
    )
    flops = 2 * 2 * win * 6 * rows * cols * width
    grad_queries, partial = pl.pallas_call(
        kernel,
        grid_spec=grid_spec,
        out_shape=[
            jax.ShapeDtypeStruct((2 * rows, cols), jnp.bfloat16),
            jax.ShapeDtypeStruct((2 * n_seq, rows, 2 * width), jnp.float32),
        ],
        compiler_params=pltpu.CompilerParams(dimension_semantics=("arbitrary",)),
        cost_estimate=pl.CostEstimate(
            flops=flops, transcendentals=2 * 2 * win * rows * cols, bytes_accessed=8 << 20
        ),
    )(blocks, doc_starts.astype(jnp.int32), srow, src_piece, dst, queries, out_grad,
      *kv_pieces, delta_t)

    storage = partial
    storage = storage.reshape(n_out, n_in, 2, rows, 2 * width)
    plane = _plane_reduce(storage, rank, n_seq, n_out, n_in, REACH)
    summed = _group_reduce(plane, n_out, "zp", 0).reshape(2 * rows, 2 * width)
    grad_keys = summed[:, :width].astype(jnp.bfloat16)
    grad_values = summed[:, width:].astype(jnp.bfloat16)
    return (grad_queries, grad_keys, grad_values)


GROUP = 4


def solution(mesh):
    n_seq, n_grp = mesh.devices.shape
    split = mesh.devices.reshape(n_seq // GROUP, GROUP, n_grp)
    mesh2 = jax.sharding.Mesh(split, ("zp", "w", "grp"))
    rows = P(("zp", "w"), "grp")
    placed = (rows, rows, rows, rows, rows, P())
    return jax.shard_map(
        body,
        mesh=mesh2,
        in_specs=placed,
        out_specs=(rows, rows, rows),
        check_vma=False,
    )
```

```python
import functools

import jax
import numpy as np
import jax.numpy as jnp
from jax import lax
from jax.experimental import pallas as pl
from jax.experimental.pallas import tpu as pltpu
from jax.sharding import PartitionSpec as P

REACH = 16


def _bwd_kernel(blk_ref, starts_ref, srow_ref, src_ref, dst_ref, q_ref, do_ref, *rest,
                rows, heads, width, reach, scaling, docs, pieces):
    kv_refs = rest[:pieces]
    (delta_ref, dq_ref, part_ref, qall, doall, dqt, kvbuf, sems, sbuf, dsbuf, qt,
     dot_t) = rest[pieces:]
    s = pl.program_id(0)
    win = reach + 1

    def copy(side, i, ref):
        row = pl.multiple_of(srow_ref[side * win + i], rows)
        return pltpu.make_async_copy(
            ref.at[pl.ds(row, rows)], kvbuf.at[side, i], sems.at[side, i]
        )

    @pl.when(s == 0)
    def _():
        for side in range(2):
            for i in range(win):
                which = src_ref[side * win + i]
                for t in range(pieces):
                    @pl.when(which == t)
                    def _():
                        copy(side, i, kv_refs[t]).start()
        part_ref[...] = jnp.zeros(part_ref.shape, jnp.float32)

    b = blk_ref[s]
    cols = heads * rows
    qpos = b * rows + lax.broadcasted_iota(jnp.int32, (1, cols), 1) % rows
    first = b * rows

    def doc_step(j, carry):
        vec, low = carry
        st = starts_ref[j]
        vec = jnp.where(st <= qpos, jnp.maximum(vec, st), vec)
        low = jnp.where(st <= first, jnp.maximum(low, st), low)
        return vec, low

    begin, low = lax.fori_loop(
        0, docs, doc_step, (jnp.zeros((1, cols), jnp.int32), jnp.int32(0))
    )
    kb0 = jnp.maximum(0, low // rows - (b - reach))
    for h in range(heads):
        q_h = q_ref[:, h * width:(h + 1) * width]
        do_h = do_ref[:, h * width:(h + 1) * width]
        qall[h * rows:(h + 1) * rows, :] = q_h
        doall[h * rows:(h + 1) * rows, :] = do_h
        qt[:, h * rows:(h + 1) * rows] = q_h.astype(jnp.float32).T.astype(jnp.bfloat16)
        dot_t[:, h * rows:(h + 1) * rows] = do_h.astype(jnp.float32).T.astype(jnp.bfloat16)
    delta = delta_ref[...]
    k_iota = lax.broadcasted_iota(jnp.int32, (rows, 1), 0)
    base = (b - reach) * rows
    nt = (((1,), (1,)), ((), ()))
    tn = (((0,), (0,)), ((), ()))
    for i in range(win):
        copy(s, i, kv_refs[0]).wait()

    def scores(c):
        kc = kvbuf[s, c, :, :width]
        st = jnp.dot(kc, qt[...], preferred_element_type=jnp.float32) * scaling
        kpos = base + c * rows + k_iota
        allowed = (kpos >= begin) & (kpos <= qpos)
        return kc, st, allowed

    def stat_step(c, m):
        _, st, allowed = scores(c)
        masked = jnp.where(allowed, st, -1e30)
        sbuf[c] = masked
        return jnp.maximum(m, jnp.max(masked, axis=0, keepdims=True))

    m0 = jnp.full((1, cols), -1e30, jnp.float32)
    l0 = jnp.zeros((1, cols), jnp.float32)
    m = lax.fori_loop(kb0, win, stat_step, m0)

    def exp_step(c, l):
        e = jnp.exp(sbuf[c] - m)
        sbuf[c] = e
        return l + jnp.sum(e, axis=0, keepdims=True)

    inv_l = 1.0 / lax.fori_loop(kb0, win, exp_step, l0)

    def grad_step(c, carry):
        p = sbuf[c] * inv_l
        vc = kvbuf[s, c, :, width:]
        dpt = jnp.dot(vc, dot_t[...], preferred_element_type=jnp.float32)
        ds = (p * (dpt - delta)).astype(jnp.bfloat16)
        pb = p.astype(jnp.bfloat16)
        dk = jnp.dot(ds, qall[...], preferred_element_type=jnp.float32) * scaling
        dv = jnp.dot(pb, doall[...], preferred_element_type=jnp.float32)
        dst = dst_ref[s * win + c]
        part_ref[dst, :, :width] += dk
        part_ref[dst, :, width:] += dv
        dsbuf[c] = ds
        return carry

    lax.fori_loop(kb0, win, grad_step, 0)

    def clear_step(c, carry):
        dsbuf[c] = jnp.zeros((rows, cols), jnp.bfloat16)
        return carry

    lax.fori_loop(0, kb0, clear_step, 0)
    kwin = kvbuf[s, :, :, :width].reshape(win * rows, width)
    dqt[...] = lax.dot_general(
        kwin, dsbuf[...].reshape(win * rows, cols), tn, preferred_element_type=jnp.float32
    )
    for h in range(heads):
        piece = dqt[:, h * rows:(h + 1) * rows]
        dq_ref[:, h * width:(h + 1) * width] = (piece.T * scaling).astype(jnp.bfloat16)


def _plane_tables(n_seq, n_out, n_in, reach):
    def needs(dp, d, slot):
        j = d if slot == 0 else 2 * n_seq - 1 - d
        up = 2 * n_seq - 1 - dp
        return (dp - reach <= j <= dp) or (up - reach <= j <= up)

    lists = {}
    for sr in range(n_seq):
        zs, ws = divmod(sr, n_in)
        for k in range(1, n_in):
            rr = zs * n_in + (ws + k) % n_in
            got = []
            for e in range(2 * n_out):
                kz, slot = divmod(e, 2)
                d = ((zs - kz) % n_out) * n_in + ws
                if needs(rr, d, slot):
                    got.append(e)
            lists[sr, k] = got
    most = max(len(v) for v in lists.values())
    send = np.zeros((n_seq, n_in - 1, most), np.int32)
    where = np.zeros((n_seq, n_in - 1, 2 * n_out), np.int32)
    for (sr, k), got in lists.items():
        padded = got + [got[0] if got else 0] * (most - len(got))
        send[sr, k - 1] = padded
        for i, e in enumerate(got):
            where[sr, k - 1, e] = i
    return most, send, where


def _partial_tables(n_seq, n_out, n_in, reach):
    def needs(dp, d, slot):
        j = d if slot == 0 else 2 * n_seq - 1 - d
        up = 2 * n_seq - 1 - dp
        return (dp - reach <= j <= dp) or (up - reach <= j <= up)

    lists = {}
    for sr in range(n_seq):
        zs, ws = divmod(sr, n_in)
        for k in range(1, n_in):
            wr = (ws + k) % n_in
            lists[sr, k] = [
                e for e in range(2 * n_out) if needs(sr, (e // 2) * n_in + wr, e % 2)
            ]
    most = max(len(v) for v in lists.values())
    send = np.zeros((n_seq, n_in - 1, most), np.int32)
    where = np.full((n_seq, n_in - 1, 2 * n_out), -1, np.int32)
    for (sr, k), got in lists.items():
        send[sr, k - 1] = got + [got[0] if got else 0] * (most - len(got))
        for i, e in enumerate(got):
            where[sr, k - 1, e] = i
    return most, send, where


def _plane_reduce(storage, rank, n_seq, n_out, n_in, reach):
    most, send_np, where_np = _partial_tables(n_seq, n_out, n_in, reach)
    me_w = lax.axis_index("w")
    me_z = lax.axis_index("zp")
    send_tab = jnp.asarray(send_np)[rank]
    where_tab = jnp.asarray(where_np)
    block = storage.shape[3:]
    total = lax.dynamic_index_in_dim(storage, me_w, 1, keepdims=False)
    total = total.reshape((2 * n_out,) + block)
    for k in range(1, n_in):
        piece = lax.dynamic_index_in_dim(storage, lax.rem(me_w + k, n_in), 1, keepdims=False)
        piece = piece.reshape((2 * n_out,) + block)
        chosen = jnp.take(piece, send_tab[k - 1], axis=0).astype(jnp.bfloat16)
        got = _shift(chosen, k, n_in, "w")
        sender = me_z * n_in + lax.rem(me_w - k + n_in, n_in)
        pos = where_tab[sender, k - 1]
        picked = jnp.take(got, jnp.maximum(pos, 0), axis=0).astype(jnp.float32)
        total = total + jnp.where((pos >= 0)[:, None, None], picked, 0.0)
    return total.reshape((n_out, 2) + block)


def _shift(x, k, n, axis):
    return lax.ppermute(x, axis, [(i, (i + k) % n) for i in range(n)])


def _group_gather(x, n, axis):
    return jnp.stack([x] + [_shift(x, k, n, axis) for k in range(1, n)])


def _group_reduce(parts, n, axis, dim):
    me = lax.axis_index(axis)
    total = lax.dynamic_index_in_dim(parts, me, dim, keepdims=False).astype(jnp.float32)
    for k in range(1, n):
        piece = lax.dynamic_index_in_dim(parts, lax.rem(me + k, n), dim, keepdims=False)
        total = total + _shift(piece.astype(jnp.bfloat16), k, n, axis).astype(jnp.float32)
    return total


def body(queries, shared_keys, shared_values, outputs, out_grad, doc_lengths):
    n_in = lax.axis_size("w")
    rank = lax.axis_index("zp") * n_in + lax.axis_index("w")
    n_out = lax.axis_size("zp")
    n_seq = n_out * n_in
    rows = shared_keys.shape[0] // 2
    width = shared_keys.shape[1]
    heads = queries.shape[1] // width
    scaling = width ** (-0.5)
    win = REACH + 1
    doc_ends = jnp.cumsum(doc_lengths)
    doc_starts = doc_ends - doc_lengths
    blocks = jnp.stack([rank, 2 * n_seq - 1 - rank]).astype(jnp.int32)

    kv_local = jnp.concatenate([shared_keys, shared_values], axis=1)
    kv_col = _group_gather(kv_local, n_out, "zp")
    most, send_np, where_np = _plane_tables(n_seq, n_out, n_in, REACH)
    send_tab = jnp.asarray(send_np)[rank]
    entries = kv_col.reshape(n_out * 2, rows, 2 * width)
    kv_pieces = [kv_col.reshape(n_out * 2 * rows, 2 * width)]
    for k in range(1, n_in):
        chosen = jnp.take(entries, send_tab[k - 1], axis=0)
        kv_pieces.append(_shift(chosen, k, n_in, "w").reshape(most * rows, 2 * width))

    me_z = lax.axis_index("zp")
    me_w = lax.axis_index("w")
    seq_blk = (blocks[:, None] - REACH + jnp.arange(win, dtype=jnp.int32)[None, :]).reshape(-1)
    seq_blk = jnp.maximum(seq_blk, 0)
    dev = jnp.where(seq_blk < n_seq, seq_blk, 2 * n_seq - 1 - seq_blk)
    slot = (seq_blk >= n_seq).astype(jnp.int32)
    k_z = lax.rem(me_z - lax.div(dev, n_in) + n_out, n_out)
    k_w = lax.rem(me_w - lax.rem(dev, n_in) + n_in, n_in)
    entry = k_z * 2 + slot
    sender = me_z * n_in + lax.rem(dev, n_in)
    pos = jnp.asarray(where_np)[sender, jnp.maximum(k_w - 1, 0), entry]
    srow = (jnp.where(k_w == 0, entry, pos) * rows).astype(jnp.int32)
    src_piece = k_w.astype(jnp.int32)
    dst = (dev * 2 + slot).astype(jnp.int32)

    prod = out_grad.astype(jnp.float32) * outputs.astype(jnp.float32)
    deltas = jnp.sum(prod.reshape(2, rows, heads, width), axis=3)
    delta_t = jnp.swapaxes(deltas, 1, 2).reshape(2, 1, heads * rows)

    kernel = functools.partial(
        _bwd_kernel, rows=rows, heads=heads, width=width, reach=REACH, scaling=scaling,
        docs=doc_lengths.shape[0], pieces=n_in,
    )
    cols = heads * rows
    vec = pl.BlockSpec((None, 1, cols), lambda s, *_: (s, 0, 0))
    grid_spec = pltpu.PrefetchScalarGridSpec(
        num_scalar_prefetch=5,
        grid=(2,),
        in_specs=[
            pl.BlockSpec((rows, cols), lambda s, *_: (s, 0)),
            pl.BlockSpec((rows, cols), lambda s, *_: (s, 0)),
        ] + [pl.BlockSpec(memory_space=pl.ANY)] * n_in + [
            vec,
        ],
        out_specs=[
            pl.BlockSpec((rows, cols), lambda s, *_: (s, 0)),
            pl.BlockSpec((2 * n_seq, rows, 2 * width), lambda s, *_: (0, 0, 0)),
        ],
        scratch_shapes=[
            pltpu.VMEM((cols, width), jnp.bfloat16),
            pltpu.VMEM((cols, width), jnp.bfloat16),
            pltpu.VMEM((width, cols), jnp.float32),
            pltpu.VMEM((2, win, rows, 2 * width), jnp.bfloat16),
            pltpu.SemaphoreType.DMA((2, win)),
            pltpu.VMEM((win, rows, cols), jnp.float32),
            pltpu.VMEM((win, rows, cols), jnp.bfloat16),
            pltpu.VMEM((width, cols), jnp.bfloat16),
            pltpu.VMEM((width, cols), jnp.bfloat16),
        ],
    )
    flops = 2 * 2 * win * 6 * rows * cols * width
    grad_queries, partial = pl.pallas_call(
        kernel,
        grid_spec=grid_spec,
        out_shape=[
            jax.ShapeDtypeStruct((2 * rows, cols), jnp.bfloat16),
            jax.ShapeDtypeStruct((2 * n_seq, rows, 2 * width), jnp.float32),
        ],
        compiler_params=pltpu.CompilerParams(dimension_semantics=("arbitrary",)),
        cost_estimate=pl.CostEstimate(
            flops=flops, transcendentals=2 * 2 * win * rows * cols, bytes_accessed=8 << 20
        ),
    )(blocks, doc_starts.astype(jnp.int32), srow, src_piece, dst, queries, out_grad,
      *kv_pieces, delta_t)

    storage = partial
    storage = storage.reshape(n_out, n_in, 2, rows, 2 * width)
    plane = _plane_reduce(storage, rank, n_seq, n_out, n_in, REACH)
    summed = _group_reduce(plane, n_out, "zp", 0).reshape(2 * rows, 2 * width)
    grad_keys = summed[:, :width].astype(jnp.bfloat16)
    grad_values = summed[:, width:].astype(jnp.bfloat16)
    return (grad_queries, grad_keys, grad_values)


GROUP = 4


def solution(mesh):
    n_seq, n_grp = mesh.devices.shape
    split = mesh.devices.reshape(n_seq // GROUP, GROUP, n_grp)
    mesh2 = jax.sharding.Mesh(split, ("zp", "w", "grp"))
    rows = P(("zp", "w"), "grp")
    placed = (rows, rows, rows, rows, rows, P())
    return jax.shard_map(
        body,
        mesh=mesh2,
        in_specs=placed,
        out_specs=(rows, rows, rows),
        check_vma=False,
    )
```
